32 devices in a mesh: group: 2 (over x), tm: 2 (over core), height: 8 (over z, y).
Axes of the slice: x: 2, y: 2, z: 4, core: 2. Of those that a mesh axis runs over, the one named last changes fastest.
Arguments:
- frames: bfloat16 [8, 16, 128, 384], P(('group', 'tm'), 'height'), parts along dimension 0, may hold values from -20 to 20
- earlier: int32 [8, 2], P(('group', 'tm')), parts along dimension 0, may hold values from -1 to 3, as said below
- gain_conv: float32 [384], replicated, may hold values from 0.1 to 1.9
- conv_weight: bfloat16 [3, 3, 3, 384, 384], replicated, may hold values from -0.0625 to 0.0625
- conv_bias: float32 [384], replicated, may hold values from -3 to 3
- gain_attn: float32 [384], replicated, may hold values from 0.1 to 1.9
- query_weight: bfloat16 [384, 384], replicated
- key_weight: bfloat16 [384, 384], replicated
- value_weight: bfloat16 [384, 384], replicated, may hold values from -0.3125 to 0.3125
- out_weight: bfloat16 [384, 384], replicated, may hold values from -0.3125 to 0.3125
Outputs:
- encoded: bfloat16 [8, 16, 128, 384], P(('group', 'tm'), 'height'), parts along dimension 0
The draws below stay inside these ranges and needn't reach their ends.
There are 2 independent parts, one for each index of `group`. The reference program is written for one: setup_inputs(seed, part) draws one part's arguments, and reference() takes and returns one part's arrays. A program takes and returns all parts, laid end to end along the dimension named above; an argument that names none is the same for every part. Nothing has to cross between parts.
Inputs may be any that keep to these rules, and one draw needn't show every extreme that they name: Row i names the spans whose frames come two back and one back before span i's frame in the same clip, -1 where the clip has no such frame; spans of a clip may lie on either index of tm, in an order drawn from the seed. earlier[i, 0] is -1 whenever earlier[i, 1] is -1. Every span is named at most once in each column.
All inputs are finite; a program needn't handle non-finite values.
Results may differ from the reference program's by a relative error of at most 0.014.
Values may be sent and summed in bfloat16 or wider, within the bound.
No kernel may reach another device: no remote copies, remote signals or barrier semaphores. Data moves between devices by JAX's collectives and lax.ppermute only.
A program may use at most 128 MiB of HBM per device.

```python
import math
import jax
import jax.numpy as jnp
from jax import lax

C = 384
W = 128
H = 16
SPANS = 4


def draw_earlier(key, part):
    order = jax.random.permutation(jax.random.fold_in(key, 1), SPANS).astype(jnp.int32)
    last_slot = jnp.argmax(order == SPANS - 1).astype(jnp.int32)
    first_value = order[0]
    order = order.at[last_slot].set(first_value).at[0].set(SPANS - 1)
    starts = jax.random.randint(jax.random.fold_in(key, 2), (SPANS,), 0, 3) == 0
    starts = starts.at[0].set(True).at[1].set(False)
    slots = jnp.arange(SPANS, dtype=jnp.int32)
    clip_begin = lax.cummax(jnp.where(starts, slots, 0), axis=0)
    position = slots - clip_begin
    back_one = jnp.where(position >= 1, jnp.roll(order, 1), -1)
    back_two = jnp.where(position >= 2, jnp.roll(order, 2), -1)
    values = jnp.stack([back_two, back_one], axis=1).astype(jnp.int32)
    return jnp.zeros((SPANS, 2), jnp.int32).at[order].set(values)


def draw_frames(key, part):
    shape = (SPANS, H, W, C)
    spread = 1.7 * jax.random.truncated_normal(jax.random.fold_in(key, 21), -4.0, 4.0, shape, jnp.float32)
    return spread.astype(jnp.bfloat16)


def query_base(key):
    return 3.0 * jax.random.truncated_normal(jax.random.fold_in(key, 11), -4.0, 4.0, (C, C), jnp.float32) / math.sqrt(C)


def draw_query_weight(key, part):
    return query_base(key).astype(jnp.bfloat16)


def draw_key_weight(key, part):
    private = jax.random.truncated_normal(jax.random.fold_in(key, 12), -4.0, 4.0, (C, C), jnp.float32) / math.sqrt(C)
    return private.astype(jnp.bfloat16)


def gaussian(rng, shape, deviation, limit, kind=jnp.bfloat16):
    drawn = deviation * jax.random.normal(rng, shape, jnp.float32)
    return jnp.clip(drawn, min=-limit, max=limit).astype(kind)


def setup_inputs(seed: int = 0, part: int = 0) -> dict:
    arg_keys = jax.random.split(jax.random.key(seed), 11)
    part_keys = jax.random.split(jax.random.fold_in(arg_keys[10], part), 11)
    return {
        "frames": draw_frames(jax.random.fold_in(jax.random.fold_in(arg_keys[10], part), 71), part),
        "earlier": draw_earlier(jax.random.fold_in(jax.random.fold_in(arg_keys[10], part), 71), part),
        "gain_conv": jnp.clip(1.0 + 0.18 * jax.random.normal(arg_keys[2], (C,), jnp.float32), 0.1, 1.9),
        "conv_weight": gaussian(arg_keys[3], (3, 3, 3, C, C), (27 * C) ** -0.5, 0.0625),
        "conv_bias": gaussian(arg_keys[4], (C,), 0.5, 3.0, jnp.float32),
        "gain_attn": jnp.clip(1.0 + 0.18 * jax.random.normal(arg_keys[5], (C,), jnp.float32), 0.1, 1.9),
        "query_weight": draw_query_weight(jax.random.fold_in(arg_keys[10], 71), part),
        "key_weight": draw_key_weight(jax.random.fold_in(arg_keys[10], 71), part),
        "value_weight": gaussian(arg_keys[8], (C, C), C ** -0.5, 0.3125),
        "out_weight": gaussian(arg_keys[9], (C, C), C ** -0.5, 0.3125),
    }


def rms_scaled(frames, gain):
    widened = frames.astype(jnp.float32)
    mean_square = lax.optimization_barrier(jnp.mean(widened * widened, axis=-1, keepdims=True))
    return widened * lax.rsqrt(mean_square + 1e-06) * gain

def reference(frames, earlier, gain_conv, conv_weight, conv_bias, gain_attn, query_weight, key_weight, value_weight, out_weight):
    activated = jax.nn.silu(rms_scaled(frames, gain_conv)).astype(jnp.bfloat16)
    padded = jnp.pad(activated, ((0, 0), (1, 1), (1, 1), (0, 0)))
    blank = jnp.zeros_like(padded[0])

    def conv_one(span_index):
        links = earlier[span_index]
        back_two = jnp.where(links[0] >= 0, padded[jnp.maximum(links[0], 0)], blank)
        back_one = jnp.where(links[1] >= 0, padded[jnp.maximum(links[1], 0)], blank)
        window = jnp.stack([back_two, back_one, padded[span_index]])
        accum = jnp.zeros((H * W, C), jnp.float32)
        for tap_t in range(3):
            for tap_y in range(3):
                for tap_x in range(3):
                    sliced = window[tap_t, tap_y:tap_y + H, tap_x:tap_x + W].reshape(H * W, C)
                    accum = accum + jnp.dot(sliced, conv_weight[tap_t, tap_y, tap_x], preferred_element_type=jnp.float32)
        return accum.reshape(H, W, C)
    conv = lax.map(conv_one, jnp.arange(SPANS, dtype=jnp.int32))
    mixed = (frames.astype(jnp.float32) + conv + conv_bias).astype(jnp.bfloat16)
    normed = rms_scaled(mixed, gain_attn).astype(jnp.bfloat16)
    score_scale = 1.0 / C ** 0.5

    def attend(tokens):
        queries = jnp.dot(tokens, query_weight, preferred_element_type=jnp.float32).astype(jnp.bfloat16)
        keys_all = jnp.dot(tokens, key_weight, preferred_element_type=jnp.float32).astype(jnp.bfloat16)
        values_all = jnp.dot(tokens, value_weight, preferred_element_type=jnp.float32).astype(jnp.bfloat16)
        scores = jnp.dot(queries, keys_all.T, preferred_element_type=jnp.float32) * score_scale
        peaks = lax.optimization_barrier(jnp.max(scores, axis=-1, keepdims=True))
        weights_exp = jnp.exp(scores - peaks)
        totals = lax.optimization_barrier(jnp.sum(weights_exp, axis=-1, keepdims=True))
        summed = jnp.dot(weights_exp.astype(jnp.bfloat16), values_all, preferred_element_type=jnp.float32)
        return (summed / totals).astype(jnp.bfloat16)
    attended = lax.map(attend, normed.reshape(SPANS, H * W, C))
    projected = jnp.dot(attended.reshape(SPANS * H * W, C), out_weight, preferred_element_type=jnp.float32)
    return (mixed.astype(jnp.float32) + projected.reshape(SPANS, H, W, C)).astype(jnp.bfloat16)
```

```python
import jax
import jax.numpy as jnp
from jax import lax
from jax.sharding import PartitionSpec as P


def padded_2(cells, sides, width):
    for axis, dim in sides:
        count = lax.axis_size(axis)
        ends = count - 1
        head = lax.slice_in_dim(cells, 0, width, axis=dim)
        tail = lax.slice_in_dim(cells, cells.shape[dim] - width, cells.shape[dim], axis=dim)
        cells = jnp.concatenate(
            [
                lax.ppermute(tail, axis, [(i, (i + 1) % count) for i in range(ends)]),
                cells,
                lax.ppermute(head, axis, [((i + 1) % count, i) for i in range(ends)]),
            ],
            axis=dim,
        )
    return cells


def rms_scaled(frames, gain):
    widened = frames.astype(jnp.float32)
    mean_square = jnp.mean(widened * widened, axis=-1, keepdims=True)
    return widened * lax.rsqrt(mean_square + 1e-06) * gain


def shards(
    frames,
    earlier,
    gain_conv,
    conv_weight,
    conv_bias,
    gain_attn,
    query_weight,
    key_weight,
    value_weight,
    out_weight,
):
    span_count, row_count, col_count, channels = frames.shape
    activated = jax.nn.silu(rms_scaled(frames, gain_conv)).astype(jnp.bfloat16)
    rimmed = padded_2(activated, (("height", 1),), 1)
    gathered = lax.all_gather(rimmed, "tm", axis=0, tiled=True)
    border = ((0, 0), (0, 0), (1, 1), (0, 0))
    padded = jnp.pad(rimmed, border)
    gathered = jnp.pad(gathered, border)
    back_two = jnp.take(gathered, jnp.maximum(earlier[:, 0], 0), axis=0)
    back_one = jnp.take(gathered, jnp.maximum(earlier[:, 1], 0), axis=0)
    present_two = (earlier[:, 0] >= 0)[:, None, None, None]
    present_one = (earlier[:, 1] >= 0)[:, None, None, None]
    back_two = jnp.where(present_two, back_two, jnp.zeros_like(back_two))
    back_one = jnp.where(present_one, back_one, jnp.zeros_like(back_one))
    window = jnp.stack([back_two, back_one, padded], axis=1)
    accum = jnp.zeros((span_count, row_count, col_count, channels), jnp.float32)
    for tap_t in range(3):
        for tap_y in range(3):
            for tap_x in range(3):
                sliced = window[:, tap_t, tap_y : tap_y + row_count, tap_x : tap_x + col_count]
                accum = accum + jnp.einsum(
                    "fhwc,cd->fhwd",
                    sliced,
                    conv_weight[tap_t, tap_y, tap_x],
                    preferred_element_type=jnp.float32,
                )
    mixed = (frames.astype(jnp.float32) + accum + conv_bias).astype(jnp.bfloat16)
    normed = rms_scaled(mixed, gain_attn).astype(jnp.bfloat16)
    tokens = normed.reshape(span_count, row_count * col_count, channels)
    queries = jnp.einsum(
        "ftc,cd->ftd", tokens, query_weight, preferred_element_type=jnp.float32
    ).astype(jnp.bfloat16)
    score_scale = 1.0 / channels**0.5
    tokens_all = lax.all_gather(tokens, "height", axis=1, tiled=True)
    keys_all = jnp.einsum(
        "ftc,cd->ftd", tokens_all, key_weight, preferred_element_type=jnp.float32
    ).astype(jnp.bfloat16)
    values_all = jnp.einsum(
        "ftc,cd->ftd", tokens_all, value_weight, preferred_element_type=jnp.float32
    ).astype(jnp.bfloat16)
    scores = (
        jnp.einsum("fqc,fkc->fqk", queries, keys_all, preferred_element_type=jnp.float32)
        * score_scale
    )
    peaks = jnp.max(scores, axis=-1, keepdims=True)
    weights_exp = jnp.exp(scores - peaks)
    totals = jnp.sum(weights_exp, axis=-1)
    summed = jnp.einsum(
        "fqk,fkc->fqc",
        weights_exp.astype(jnp.bfloat16),
        values_all,
        preferred_element_type=jnp.float32,
    )
    attended = (summed / totals[:, :, None]).astype(jnp.bfloat16)
    projected = jnp.einsum("ftc,cd->ftd", attended, out_weight, preferred_element_type=jnp.float32)
    encoded = mixed.astype(jnp.float32) + projected.reshape(
        span_count, row_count, col_count, channels
    )
    return encoded.astype(jnp.bfloat16)


def solution(mesh):
    in_specs = (
        P(("group", "tm"), "height", None, None),
        P(("group", "tm"), None),
        P(),
        P(),
        P(),
        P(),
        P(),
        P(),
        P(),
        P(),
    )
    out_specs = P(("group", "tm"), "height", None, None)
    return jax.shard_map(shards, mesh=mesh, in_specs=in_specs, out_specs=out_specs, check_vma=False)
```

```python
import jax
import jax.numpy as jnp
from jax import lax
from jax.sharding import PartitionSpec as P


def padded_2(cells, sides, width):
    for axis, dim in sides:
        count = lax.axis_size(axis)
        ends = count - 1
        head = lax.slice_in_dim(cells, 0, width, axis=dim)
        tail = lax.slice_in_dim(cells, cells.shape[dim] - width, cells.shape[dim], axis=dim)
        cells = jnp.concatenate(
            [
                lax.ppermute(tail, axis, [(i, (i + 1) % count) for i in range(ends)]),
                cells,
                lax.ppermute(head, axis, [((i + 1) % count, i) for i in range(ends)]),
            ],
            axis=dim,
        )
    return cells


def rms_scaled(frames, gain):
    widened = frames.astype(jnp.float32)
    mean_square = jnp.mean(widened * widened, axis=-1, keepdims=True)
    return widened * lax.rsqrt(mean_square + 1e-06) * gain


def shards(
    frames,
    earlier,
    gain_conv,
    conv_weight,
    conv_bias,
    gain_attn,
    query_weight,
    key_weight,
    value_weight,
    out_weight,
):
    span_count, row_count, col_count, channels = frames.shape
    activated = jax.nn.silu(rms_scaled(frames, gain_conv)).astype(jnp.bfloat16)
    rimmed = padded_2(activated, (("height", 1),), 1)
    gathered = lax.all_gather(rimmed, "tm", axis=0, tiled=True)
    border = ((0, 0), (0, 0), (1, 1), (0, 0))
    padded = jnp.pad(rimmed, border)
    gathered = jnp.pad(gathered, border)
    back_two = jnp.take(gathered, jnp.maximum(earlier[:, 0], 0), axis=0)
    back_one = jnp.take(gathered, jnp.maximum(earlier[:, 1], 0), axis=0)
    present_two = (earlier[:, 0] >= 0)[:, None, None, None]
    present_one = (earlier[:, 1] >= 0)[:, None, None, None]
    back_two = jnp.where(present_two, back_two, jnp.zeros_like(back_two))
    back_one = jnp.where(present_one, back_one, jnp.zeros_like(back_one))
    window = jnp.stack([back_two, back_one, padded], axis=1)
    score_scale = 1.0 / channels**0.5

    def conv_span(span_window, span):
        accum = jnp.zeros((row_count, col_count, channels), jnp.float32)
        for tap_t in range(3):
            for tap_y in range(3):
                for tap_x in range(3):
                    sliced = span_window[tap_t, tap_y : tap_y + row_count, tap_x : tap_x + col_count]
                    accum = accum + jnp.einsum(
                        "hwc,cd->hwd",
                        sliced,
                        conv_weight[tap_t, tap_y, tap_x],
                        preferred_element_type=jnp.float32,
                    )
        mixed = (frames[span].astype(jnp.float32) + accum + conv_bias).astype(jnp.bfloat16)
        normed = rms_scaled(mixed, gain_attn).astype(jnp.bfloat16)
        return mixed, normed.reshape(row_count * col_count, channels)

    def attend_span(mixed, tokens, tokens_all):
        queries = jnp.dot(tokens, query_weight, preferred_element_type=jnp.float32).astype(
            jnp.bfloat16
        )
        keys_all = jnp.dot(tokens_all, key_weight, preferred_element_type=jnp.float32).astype(
            jnp.bfloat16
        )
        values_all = jnp.dot(
            tokens_all, value_weight, preferred_element_type=jnp.float32
        ).astype(jnp.bfloat16)
        scores = (
            jnp.einsum("qc,kc->qk", queries, keys_all, preferred_element_type=jnp.float32)
            * score_scale
        )
        peaks = jnp.max(scores, axis=-1, keepdims=True)
        weights_exp = jnp.exp(scores - peaks)
        totals = jnp.sum(weights_exp, axis=-1, keepdims=True)
        summed = jnp.dot(
            weights_exp.astype(jnp.bfloat16), values_all, preferred_element_type=jnp.float32
        )
        attended = (summed / totals).astype(jnp.bfloat16)
        projected = jnp.dot(attended, out_weight, preferred_element_type=jnp.float32)
        encoded = mixed.astype(jnp.float32) + projected.reshape(row_count, col_count, channels)
        return encoded.astype(jnp.bfloat16)

    outputs = []
    pending = None
    span_window = window[0]
    for span in range(span_count):
        mixed, tokens = conv_span(span_window, span)
        if span + 1 < span_count:
            tokens, span_window = lax.optimization_barrier((tokens, window[span + 1]))
        tokens_all = lax.all_gather(tokens, "height", axis=0, tiled=True)
        if pending is not None:
            mixed, tokens, pending = lax.optimization_barrier((mixed, tokens, pending))
            outputs.append(attend_span(*pending))
        pending = (mixed, tokens, tokens_all)
    outputs.append(attend_span(*pending))
    return jnp.stack(outputs, axis=0)


def solution(mesh):
    in_specs = (
        P(("group", "tm"), "height", None, None),
        P(("group", "tm"), None),
        P(),
        P(),
        P(),
        P(),
        P(),
        P(),
        P(),
        P(),
    )
    out_specs = P(("group", "tm"), "height", None, None)
    return jax.shard_map(shards, mesh=mesh, in_specs=in_specs, out_specs=out_specs, check_vma=False)
```

```python
import jax
import jax.numpy as jnp
from jax import lax
from jax.sharding import PartitionSpec as P


def padded_2(cells, sides, width):
    for axis, dim in sides:
        count = lax.axis_size(axis)
        ends = count - 1
        head = lax.slice_in_dim(cells, 0, width, axis=dim)
        tail = lax.slice_in_dim(cells, cells.shape[dim] - width, cells.shape[dim], axis=dim)
        cells = jnp.concatenate(
            [
                lax.ppermute(tail, axis, [(i, (i + 1) % count) for i in range(ends)]),
                cells,
                lax.ppermute(head, axis, [((i + 1) % count, i) for i in range(ends)]),
            ],
            axis=dim,
        )
    return cells


def ring_gather(block, axis, dim):
    count = lax.axis_size(axis)
    ring = list(range(0, count, 2)) + list(range(count - 1 - count % 2, 0, -2))
    ahead = [(ring[p], ring[(p + 1) % count]) for p in range(count)]
    behind = [(ring[p], ring[(p - 1) % count]) for p in range(count)]
    pieces = [block]
    forward = block
    backward = block
    for step in range(count // 2):
        forward = lax.ppermute(forward, axis, ahead)
        pieces.append(forward)
        if len(pieces) < count:
            backward = lax.ppermute(backward, axis, behind)
            pieces.append(backward)
    return jnp.concatenate(pieces, axis=dim)


def rms_scaled(frames, gain):
    widened = frames.astype(jnp.float32)
    mean_square = jnp.mean(widened * widened, axis=-1, keepdims=True)
    return widened * lax.rsqrt(mean_square + 1e-06) * gain


def shards(
    frames,
    earlier,
    gain_conv,
    conv_weight,
    conv_bias,
    gain_attn,
    query_weight,
    key_weight,
    value_weight,
    out_weight,
):
    span_count, row_count, col_count, channels = frames.shape
    activated = jax.nn.silu(rms_scaled(frames, gain_conv)).astype(jnp.bfloat16)
    rimmed = padded_2(activated, (("height", 1),), 1)
    gathered = lax.all_gather(rimmed, "tm", axis=0, tiled=True)
    border = ((0, 0), (0, 0), (1, 1), (0, 0))
    padded = jnp.pad(rimmed, border)
    gathered = jnp.pad(gathered, border)
    back_two = jnp.take(gathered, jnp.maximum(earlier[:, 0], 0), axis=0)
    back_one = jnp.take(gathered, jnp.maximum(earlier[:, 1], 0), axis=0)
    present_two = (earlier[:, 0] >= 0)[:, None, None, None]
    present_one = (earlier[:, 1] >= 0)[:, None, None, None]
    back_two = jnp.where(present_two, back_two, jnp.zeros_like(back_two))
    back_one = jnp.where(present_one, back_one, jnp.zeros_like(back_one))
    window = jnp.stack([back_two, back_one, padded], axis=1)
    accum = jnp.zeros((span_count, row_count, col_count, channels), jnp.float32)
    for tap_t in range(3):
        for tap_y in range(3):
            for tap_x in range(3):
                sliced = window[:, tap_t, tap_y : tap_y + row_count, tap_x : tap_x + col_count]
                accum = accum + jnp.einsum(
                    "fhwc,cd->fhwd",
                    sliced,
                    conv_weight[tap_t, tap_y, tap_x],
                    preferred_element_type=jnp.float32,
                )
    mixed = (frames.astype(jnp.float32) + accum + conv_bias).astype(jnp.bfloat16)
    normed = rms_scaled(mixed, gain_attn).astype(jnp.bfloat16)
    tokens = normed.reshape(span_count, row_count * col_count, channels)
    queries = jnp.einsum(
        "ftc,cd->ftd", tokens, query_weight, preferred_element_type=jnp.float32
    ).astype(jnp.bfloat16)
    score_scale = 1.0 / channels**0.5
    tokens_all = ring_gather(tokens, "height", 1)
    keys_all = jnp.einsum(
        "ftc,cd->ftd", tokens_all, key_weight, preferred_element_type=jnp.float32
    ).astype(jnp.bfloat16)
    values_all = jnp.einsum(
        "ftc,cd->ftd", tokens_all, value_weight, preferred_element_type=jnp.float32
    ).astype(jnp.bfloat16)
    scores = (
        jnp.einsum("fqc,fkc->fqk", queries, keys_all, preferred_element_type=jnp.float32)
        * score_scale
    )
    peaks = jnp.max(scores, axis=-1, keepdims=True)
    weights_exp = jnp.exp(scores - peaks)
    totals = jnp.sum(weights_exp, axis=-1)
    summed = jnp.einsum(
        "fqk,fkc->fqc",
        weights_exp.astype(jnp.bfloat16),
        values_all,
        preferred_element_type=jnp.float32,
    )
    attended = (summed / totals[:, :, None]).astype(jnp.bfloat16)
    projected = jnp.einsum("ftc,cd->ftd", attended, out_weight, preferred_element_type=jnp.float32)
    encoded = mixed.astype(jnp.float32) + projected.reshape(
        span_count, row_count, col_count, channels
    )
    return encoded.astype(jnp.bfloat16)


def solution(mesh):
    in_specs = (
        P(("group", "tm"), "height", None, None),
        P(("group", "tm"), None),
        P(),
        P(),
        P(),
        P(),
        P(),
        P(),
        P(),
        P(),
    )
    out_specs = P(("group", "tm"), "height", None, None)
    return jax.shard_map(shards, mesh=mesh, in_specs=in_specs, out_specs=out_specs, check_vma=False)
```

```python
import jax
import jax.numpy as jnp
from jax import lax
from jax.sharding import PartitionSpec as P


def padded_2(cells, sides, width):
    for axis, dim in sides:
        count = lax.axis_size(axis)
        ends = count - 1
        head = lax.slice_in_dim(cells, 0, width, axis=dim)
        tail = lax.slice_in_dim(cells, cells.shape[dim] - width, cells.shape[dim], axis=dim)
        cells = jnp.concatenate(
            [
                lax.ppermute(tail, axis, [(i, (i + 1) % count) for i in range(ends)]),
                cells,
                lax.ppermute(head, axis, [((i + 1) % count, i) for i in range(ends)]),
            ],
            axis=dim,
        )
    return cells


def ring_gather(block, axis, dim):
    count = lax.axis_size(axis)
    ring = list(range(0, count, 2)) + list(range(count - 1 - count % 2, 0, -2))
    ahead = [(ring[p], ring[(p + 1) % count]) for p in range(count)]
    behind = [(ring[p], ring[(p - 1) % count]) for p in range(count)]
    pieces = [block]
    forward = block
    backward = block
    for step in range(count // 2):
        forward = lax.ppermute(forward, axis, ahead)
        pieces.append(forward)
        if len(pieces) < count:
            backward = lax.ppermute(backward, axis, behind)
            pieces.append(backward)
    return jnp.concatenate(pieces, axis=dim)


def rms_scaled(frames, gain):
    widened = frames.astype(jnp.float32)
    mean_square = jnp.mean(widened * widened, axis=-1, keepdims=True)
    return widened * lax.rsqrt(mean_square + 1e-06) * gain


def shards(
    frames,
    earlier,
    gain_conv,
    conv_weight,
    conv_bias,
    gain_attn,
    query_weight,
    key_weight,
    value_weight,
    out_weight,
):
    span_count, row_count, col_count, channels = frames.shape
    activated = jax.nn.silu(rms_scaled(frames, gain_conv)).astype(jnp.bfloat16)
    rimmed = padded_2(activated, (("height", 1),), 1)
    gathered = lax.all_gather(rimmed, "tm", axis=0, tiled=True)
    border = ((0, 0), (0, 0), (1, 1), (0, 0))
    padded = jnp.pad(rimmed, border)
    gathered = jnp.pad(gathered, border)
    back_two = jnp.take(gathered, jnp.maximum(earlier[:, 0], 0), axis=0)
    back_one = jnp.take(gathered, jnp.maximum(earlier[:, 1], 0), axis=0)
    present_two = (earlier[:, 0] >= 0)[:, None, None, None]
    present_one = (earlier[:, 1] >= 0)[:, None, None, None]
    back_two = jnp.where(present_two, back_two, jnp.zeros_like(back_two))
    back_one = jnp.where(present_one, back_one, jnp.zeros_like(back_one))
    window = jnp.stack([back_two, back_one, padded], axis=1)
    accum = lax.conv_general_dilated(
        window,
        conv_weight,
        window_strides=(1, 1, 1),
        padding="VALID",
        dimension_numbers=("NDHWC", "DHWIO", "NDHWC"),
        preferred_element_type=jnp.float32,
    )[:, 0]
    mixed = (frames.astype(jnp.float32) + accum + conv_bias).astype(jnp.bfloat16)
    normed = rms_scaled(mixed, gain_attn).astype(jnp.bfloat16)
    tokens = normed.reshape(span_count, row_count * col_count, channels)
    queries = jnp.einsum(
        "ftc,cd->ftd", tokens, query_weight, preferred_element_type=jnp.float32
    ).astype(jnp.bfloat16)
    score_scale = 1.0 / channels**0.5
    tokens_all = ring_gather(tokens, "height", 1)
    keys_all = jnp.einsum(
        "ftc,cd->ftd", tokens_all, key_weight, preferred_element_type=jnp.float32
    ).astype(jnp.bfloat16)
    values_all = jnp.einsum(
        "ftc,cd->ftd", tokens_all, value_weight, preferred_element_type=jnp.float32
    ).astype(jnp.bfloat16)
    scores = (
        jnp.einsum("fqc,fkc->fqk", queries, keys_all, preferred_element_type=jnp.float32)
        * score_scale
    )
    peaks = jnp.max(scores, axis=-1, keepdims=True)
    weights_exp = jnp.exp(scores - peaks)
    totals = jnp.sum(weights_exp, axis=-1)
    summed = jnp.einsum(
        "fqk,fkc->fqc",
        weights_exp.astype(jnp.bfloat16),
        values_all,
        preferred_element_type=jnp.float32,
    )
    attended = (summed / totals[:, :, None]).astype(jnp.bfloat16)
    projected = jnp.einsum("ftc,cd->ftd", attended, out_weight, preferred_element_type=jnp.float32)
    encoded = mixed.astype(jnp.float32) + projected.reshape(
        span_count, row_count, col_count, channels
    )
    return encoded.astype(jnp.bfloat16)


def solution(mesh):
    in_specs = (
        P(("group", "tm"), "height", None, None),
        P(("group", "tm"), None),
        P(),
        P(),
        P(),
        P(),
        P(),
        P(),
        P(),
        P(),
    )
    out_specs = P(("group", "tm"), "height", None, None)
    return jax.shard_map(shards, mesh=mesh, in_specs=in_specs, out_specs=out_specs, check_vma=False)
```

```python
import jax
import jax.numpy as jnp
from jax import lax
from jax.sharding import PartitionSpec as P


def padded_2(cells, sides, width):
    for axis, dim in sides:
        count = lax.axis_size(axis)
        ends = count - 1
        head = lax.slice_in_dim(cells, 0, width, axis=dim)
        tail = lax.slice_in_dim(cells, cells.shape[dim] - width, cells.shape[dim], axis=dim)
        cells = jnp.concatenate(
            [
                lax.ppermute(tail, axis, [(i, (i + 1) % count) for i in range(ends)]),
                cells,
                lax.ppermute(head, axis, [((i + 1) % count, i) for i in range(ends)]),
            ],
            axis=dim,
        )
    return cells


def ring_gather(block, axis, dim):
    count = lax.axis_size(axis)
    ring = list(range(0, count, 2)) + list(range(count - 1 - count % 2, 0, -2))
    ahead = [(ring[p], ring[(p + 1) % count]) for p in range(count)]
    behind = [(ring[p], ring[(p - 1) % count]) for p in range(count)]
    pieces = [block]
    forward = block
    backward = block
    for step in range((count - 1) // 2):
        forward = lax.ppermute(forward, axis, ahead)
        backward = lax.ppermute(backward, axis, behind)
        pieces += [forward, backward]
    if count % 2 == 0 and count > 1:
        half = block.shape[dim] // 2
        front = lax.ppermute(lax.slice_in_dim(forward, 0, half, axis=dim), axis, ahead)
        back = lax.ppermute(
            lax.slice_in_dim(backward, half, block.shape[dim], axis=dim), axis, behind
        )
        pieces += [front, back]
    return jnp.concatenate(pieces, axis=dim)


def rms_scaled(frames, gain):
    widened = frames.astype(jnp.float32)
    mean_square = jnp.mean(widened * widened, axis=-1, keepdims=True)
    return widened * lax.rsqrt(mean_square + 1e-06) * gain


def shards(
    frames,
    earlier,
    gain_conv,
    conv_weight,
    conv_bias,
    gain_attn,
    query_weight,
    key_weight,
    value_weight,
    out_weight,
):
    span_count, row_count, col_count, channels = frames.shape
    activated = jax.nn.silu(rms_scaled(frames, gain_conv)).astype(jnp.bfloat16)
    rimmed = padded_2(activated, (("height", 1),), 1)
    gathered = lax.all_gather(rimmed, "tm", axis=0, tiled=True)
    border = ((0, 0), (0, 0), (1, 1), (0, 0))
    padded = jnp.pad(rimmed, border)
    gathered = jnp.pad(gathered, border)
    back_two = jnp.take(gathered, jnp.maximum(earlier[:, 0], 0), axis=0)
    back_one = jnp.take(gathered, jnp.maximum(earlier[:, 1], 0), axis=0)
    present_two = (earlier[:, 0] >= 0)[:, None, None, None]
    present_one = (earlier[:, 1] >= 0)[:, None, None, None]
    back_two = jnp.where(present_two, back_two, jnp.zeros_like(back_two))
    back_one = jnp.where(present_one, back_one, jnp.zeros_like(back_one))
    window = jnp.stack([back_two, back_one, padded], axis=1)
    accum = lax.conv_general_dilated(
        window,
        conv_weight,
        window_strides=(1, 1, 1),
        padding="VALID",
        dimension_numbers=("NDHWC", "DHWIO", "NDHWC"),
        preferred_element_type=jnp.float32,
    )[:, 0]
    mixed = (frames.astype(jnp.float32) + accum + conv_bias).astype(jnp.bfloat16)
    normed = rms_scaled(mixed, gain_attn).astype(jnp.bfloat16)
    tokens = normed.reshape(span_count, row_count * col_count, channels)
    queries = jnp.einsum(
        "ftc,cd->ftd", tokens, query_weight, preferred_element_type=jnp.float32
    ).astype(jnp.bfloat16)
    score_scale = 1.0 / channels**0.5
    tokens_all = ring_gather(tokens, "height", 1)
    keys_all = jnp.einsum(
        "ftc,cd->ftd", tokens_all, key_weight, preferred_element_type=jnp.float32
    ).astype(jnp.bfloat16)
    values_all = jnp.einsum(
        "ftc,cd->ftd", tokens_all, value_weight, preferred_element_type=jnp.float32
    ).astype(jnp.bfloat16)
    scores = (
        jnp.einsum("fqc,fkc->fqk", queries, keys_all, preferred_element_type=jnp.float32)
        * score_scale
    )
    peaks = jnp.max(scores, axis=-1, keepdims=True)
    weights_exp = jnp.exp(scores - peaks)
    totals = jnp.sum(weights_exp, axis=-1)
    summed = jnp.einsum(
        "fqk,fkc->fqc",
        weights_exp.astype(jnp.bfloat16),
        values_all,
        preferred_element_type=jnp.float32,
    )
    attended = (summed / totals[:, :, None]).astype(jnp.bfloat16)
    projected = jnp.einsum("ftc,cd->ftd", attended, out_weight, preferred_element_type=jnp.float32)
    encoded = mixed.astype(jnp.float32) + projected.reshape(
        span_count, row_count, col_count, channels
    )
    return encoded.astype(jnp.bfloat16)


def solution(mesh):
    in_specs = (
        P(("group", "tm"), "height", None, None),
        P(("group", "tm"), None),
        P(),
        P(),
        P(),
        P(),
        P(),
        P(),
        P(),
        P(),
    )
    out_specs = P(("group", "tm"), "height", None, None)
    return jax.shard_map(shards, mesh=mesh, in_specs=in_specs, out_specs=out_specs, check_vma=False)
```

```python
import jax
import jax.numpy as jnp
from jax import lax
from jax.sharding import PartitionSpec as P


def padded_2(cells, sides, width):
    for axis, dim in sides:
        count = lax.axis_size(axis)
        ends = count - 1
        head = lax.slice_in_dim(cells, 0, width, axis=dim)
        tail = lax.slice_in_dim(cells, cells.shape[dim] - width, cells.shape[dim], axis=dim)
        cells = jnp.concatenate(
            [
                lax.ppermute(tail, axis, [(i, (i + 1) % count) for i in range(ends)]),
                cells,
                lax.ppermute(head, axis, [((i + 1) % count, i) for i in range(ends)]),
            ],
            axis=dim,
        )
    return cells


def ring_gather(block, axis, dim):
    count = lax.axis_size(axis)
    ring = list(range(0, count, 2)) + list(range(count - 1 - count % 2, 0, -2))
    ahead = [(ring[p], ring[(p + 1) % count]) for p in range(count)]
    behind = [(ring[p], ring[(p - 1) % count]) for p in range(count)]
    pieces = [block]
    forward = block
    backward = block
    for step in range((count - 1) // 2):
        forward = lax.ppermute(forward, axis, ahead)
        backward = lax.ppermute(backward, axis, behind)
        pieces += [forward, backward]
    if count % 2 == 0 and count > 1:
        half = block.shape[dim] // 2
        front = lax.ppermute(lax.slice_in_dim(forward, 0, half, axis=dim), axis, ahead)
        back = lax.ppermute(
            lax.slice_in_dim(backward, half, block.shape[dim], axis=dim), axis, behind
        )
        pieces += [front, back]
    return jnp.concatenate(pieces, axis=dim)


def rms_scaled(frames, gain):
    widened = frames.astype(jnp.float32)
    mean_square = jnp.mean(widened * widened, axis=-1, keepdims=True)
    return widened * lax.rsqrt(mean_square + 1e-06) * gain


def shards(
    frames,
    earlier,
    gain_conv,
    conv_weight,
    conv_bias,
    gain_attn,
    query_weight,
    key_weight,
    value_weight,
    out_weight,
):
    span_count, row_count, col_count, channels = frames.shape
    activated = jax.nn.silu(rms_scaled(frames, gain_conv)).astype(jnp.bfloat16)
    activated = jnp.pad(activated, ((0, 0), (0, 0), (1, 1), (0, 0)))
    rimmed = padded_2(activated, (("height", 1),), 1)
    ways = lax.axis_size("tm")
    mine = lax.axis_index("tm")
    pieces = [rimmed]
    for shift in range(1, ways):
        pieces.append(
            lax.ppermute(rimmed, "tm", [(i, (i + shift) % ways) for i in range(ways)])
        )
    pieces.append(jnp.zeros_like(rimmed[:1]))
    pool = jnp.concatenate(pieces, axis=0)
    blank = ways * span_count

    def slot(index):
        place = ((mine - index // span_count) % ways) * span_count + index % span_count
        return jnp.where(index >= 0, place, blank)

    own = jnp.arange(span_count, dtype=earlier.dtype)
    picks = jnp.stack([slot(earlier[:, 0]), slot(earlier[:, 1]), own], axis=1)
    window = jnp.take(pool, picks.reshape(-1), axis=0).reshape(
        (span_count, 3) + rimmed.shape[1:]
    )
    accum = lax.conv_general_dilated(
        window,
        conv_weight,
        window_strides=(1, 1, 1),
        padding="VALID",
        dimension_numbers=("NDHWC", "DHWIO", "NDHWC"),
        preferred_element_type=jnp.float32,
    )[:, 0]
    mixed = (frames.astype(jnp.float32) + accum + conv_bias).astype(jnp.bfloat16)
    normed = rms_scaled(mixed, gain_attn).astype(jnp.bfloat16)
    tokens = normed.reshape(span_count, row_count * col_count, channels)
    queries = jnp.einsum(
        "ftc,cd->ftd", tokens, query_weight, preferred_element_type=jnp.float32
    ).astype(jnp.bfloat16)
    score_scale = 1.0 / channels**0.5
    tokens_all = ring_gather(tokens, "height", 1)
    keys_all = jnp.einsum(
        "ftc,cd->ftd", tokens_all, key_weight, preferred_element_type=jnp.float32
    ).astype(jnp.bfloat16)
    values_all = jnp.einsum(
        "ftc,cd->ftd", tokens_all, value_weight, preferred_element_type=jnp.float32
    ).astype(jnp.bfloat16)
    scores = (
        jnp.einsum("fqc,fkc->fqk", queries, keys_all, preferred_element_type=jnp.float32)
        * score_scale
    )
    peaks = jnp.max(scores, axis=-1, keepdims=True)
    weights_exp = jnp.exp(scores - peaks)
    totals = jnp.sum(weights_exp, axis=-1)
    summed = jnp.einsum(
        "fqk,fkc->fqc",
        weights_exp.astype(jnp.bfloat16),
        values_all,
        preferred_element_type=jnp.float32,
    )
    attended = (summed / totals[:, :, None]).astype(jnp.bfloat16)
    projected = jnp.einsum("ftc,cd->ftd", attended, out_weight, preferred_element_type=jnp.float32)
    encoded = mixed.astype(jnp.float32) + projected.reshape(
        span_count, row_count, col_count, channels
    )
    return encoded.astype(jnp.bfloat16)


def solution(mesh):
    in_specs = (
        P(("group", "tm"), "height", None, None),
        P(("group", "tm"), None),
        P(),
        P(),
        P(),
        P(),
        P(),
        P(),
        P(),
        P(),
    )
    out_specs = P(("group", "tm"), "height", None, None)
    return jax.shard_map(shards, mesh=mesh, in_specs=in_specs, out_specs=out_specs, check_vma=False)
```

```python
import jax
import jax.numpy as jnp
from jax import lax
from jax.sharding import PartitionSpec as P


def padded_2(cells, sides, width):
    for axis, dim in sides:
        count = lax.axis_size(axis)
        ends = count - 1
        head = lax.slice_in_dim(cells, 0, width, axis=dim)
        tail = lax.slice_in_dim(cells, cells.shape[dim] - width, cells.shape[dim], axis=dim)
        cells = jnp.concatenate(
            [
                lax.ppermute(tail, axis, [(i, (i + 1) % count) for i in range(ends)]),
                cells,
                lax.ppermute(head, axis, [((i + 1) % count, i) for i in range(ends)]),
            ],
            axis=dim,
        )
    return cells


def ring_gather(block, axis, dim):
    count = lax.axis_size(axis)
    ring = list(range(0, count, 2)) + list(range(count - 1 - count % 2, 0, -2))
    ahead = [(ring[p], ring[(p + 1) % count]) for p in range(count)]
    behind = [(ring[p], ring[(p - 1) % count]) for p in range(count)]
    pieces = [block]
    forward = block
    backward = block
    for step in range((count - 1) // 2):
        forward = lax.ppermute(forward, axis, ahead)
        backward = lax.ppermute(backward, axis, behind)
        pieces += [forward, backward]
    if count % 2 == 0 and count > 1:
        half = block.shape[dim] // 2
        front = lax.ppermute(lax.slice_in_dim(forward, 0, half, axis=dim), axis, ahead)
        back = lax.ppermute(
            lax.slice_in_dim(backward, half, block.shape[dim], axis=dim), axis, behind
        )
        pieces += [front, back]
    return pieces


def rms_scaled(frames, gain):
    widened = frames.astype(jnp.float32)
    mean_square = jnp.mean(widened * widened, axis=-1, keepdims=True)
    return widened * lax.rsqrt(mean_square + 1e-06) * gain


def shards(
    frames,
    earlier,
    gain_conv,
    conv_weight,
    conv_bias,
    gain_attn,
    query_weight,
    key_weight,
    value_weight,
    out_weight,
):
    span_count, row_count, col_count, channels = frames.shape
    activated = jax.nn.silu(rms_scaled(frames, gain_conv)).astype(jnp.bfloat16)
    activated = jnp.pad(activated, ((0, 0), (0, 0), (1, 1), (0, 0)))
    rimmed = padded_2(activated, (("height", 1),), 1)
    ways = lax.axis_size("tm")
    mine = lax.axis_index("tm")
    pieces = [rimmed]
    for shift in range(1, ways):
        pieces.append(
            lax.ppermute(rimmed, "tm", [(i, (i + shift) % ways) for i in range(ways)])
        )
    pieces.append(jnp.zeros_like(rimmed[:1]))
    pool = jnp.concatenate(pieces, axis=0)
    blank = ways * span_count

    def slot(index):
        place = ((mine - index // span_count) % ways) * span_count + index % span_count
        return jnp.where(index >= 0, place, blank)

    own = jnp.arange(span_count, dtype=earlier.dtype)
    picks = jnp.stack([slot(earlier[:, 0]), slot(earlier[:, 1]), own], axis=1)
    window = jnp.take(pool, picks.reshape(-1), axis=0).reshape(
        (span_count, 3) + rimmed.shape[1:]
    )
    accum = lax.conv_general_dilated(
        window,
        conv_weight,
        window_strides=(1, 1, 1),
        padding="VALID",
        dimension_numbers=("NDHWC", "DHWIO", "NDHWC"),
        preferred_element_type=jnp.float32,
    )[:, 0]
    mixed = (frames.astype(jnp.float32) + accum + conv_bias).astype(jnp.bfloat16)
    normed = rms_scaled(mixed, gain_attn).astype(jnp.bfloat16)
    tokens = normed.reshape(span_count, row_count * col_count, channels)
    queries = jnp.einsum(
        "ftc,cd->ftd", tokens, query_weight, preferred_element_type=jnp.float32
    ).astype(jnp.bfloat16)
    score_scale = 1.0 / channels**0.5
    pieces = ring_gather(tokens, "height", 1)
    scored = []
    for piece in pieces:
        keys = jnp.einsum(
            "ftc,cd->ftd", piece, key_weight, preferred_element_type=jnp.float32
        ).astype(jnp.bfloat16)
        values = jnp.einsum(
            "ftc,cd->ftd", piece, value_weight, preferred_element_type=jnp.float32
        ).astype(jnp.bfloat16)
        scores = (
            jnp.einsum("fqc,fkc->fqk", queries, keys, preferred_element_type=jnp.float32)
            * score_scale
        )
        scored.append((scores, values))
    peaks = scored[0][0].max(axis=-1, keepdims=True)
    for scores, _ in scored[1:]:
        peaks = jnp.maximum(peaks, scores.max(axis=-1, keepdims=True))
    totals = None
    summed = None
    for scores, values in scored:
        weights_exp = jnp.exp(scores - peaks)
        part_total = jnp.sum(weights_exp, axis=-1)
        part_sum = jnp.einsum(
            "fqk,fkc->fqc",
            weights_exp.astype(jnp.bfloat16),
            values,
            preferred_element_type=jnp.float32,
        )
        totals = part_total if totals is None else totals + part_total
        summed = part_sum if summed is None else summed + part_sum
    attended = (summed / totals[:, :, None]).astype(jnp.bfloat16)
    projected = jnp.einsum("ftc,cd->ftd", attended, out_weight, preferred_element_type=jnp.float32)
    encoded = mixed.astype(jnp.float32) + projected.reshape(
        span_count, row_count, col_count, channels
    )
    return encoded.astype(jnp.bfloat16)


def solution(mesh):
    in_specs = (
        P(("group", "tm"), "height", None, None),
        P(("group", "tm"), None),
        P(),
        P(),
        P(),
        P(),
        P(),
        P(),
        P(),
        P(),
    )
    out_specs = P(("group", "tm"), "height", None, None)
    return jax.shard_map(shards, mesh=mesh, in_specs=in_specs, out_specs=out_specs, check_vma=False)
```

```python
import jax
import jax.numpy as jnp
from jax import lax
from jax.experimental import pallas as pl
from jax.sharding import PartitionSpec as P


def padded_2(cells, sides, width):
    for axis, dim in sides:
        count = lax.axis_size(axis)
        ends = count - 1
        head = lax.slice_in_dim(cells, 0, width, axis=dim)
        tail = lax.slice_in_dim(cells, cells.shape[dim] - width, cells.shape[dim], axis=dim)
        cells = jnp.concatenate(
            [
                lax.ppermute(tail, axis, [(i, (i + 1) % count) for i in range(ends)]),
                cells,
                lax.ppermute(head, axis, [((i + 1) % count, i) for i in range(ends)]),
            ],
            axis=dim,
        )
    return cells


def ring_gather(block, axis, dim):
    count = lax.axis_size(axis)
    ring = list(range(0, count, 2)) + list(range(count - 1 - count % 2, 0, -2))
    ahead = [(ring[p], ring[(p + 1) % count]) for p in range(count)]
    behind = [(ring[p], ring[(p - 1) % count]) for p in range(count)]
    pieces = [block]
    forward = block
    backward = block
    for step in range((count - 1) // 2):
        forward = lax.ppermute(forward, axis, ahead)
        backward = lax.ppermute(backward, axis, behind)
        pieces += [forward, backward]
    if count % 2 == 0 and count > 1:
        half = block.shape[dim] // 2
        front = lax.ppermute(lax.slice_in_dim(forward, 0, half, axis=dim), axis, ahead)
        back = lax.ppermute(
            lax.slice_in_dim(backward, half, block.shape[dim], axis=dim), axis, behind
        )
        pieces += [front, back]
    return jnp.concatenate(pieces, axis=dim)


def attend_kernel(query_ref, key_ref, value_ref, out_ref, *, scale):
    scores = (
        lax.dot_general(
            query_ref[0],
            key_ref[0],
            (((1,), (1,)), ((), ())),
            preferred_element_type=jnp.float32,
        )
        * scale
    )
    peaks = jnp.max(scores, axis=-1, keepdims=True)
    weights_exp = jnp.exp(scores - peaks)
    totals = jnp.sum(weights_exp, axis=-1, keepdims=True)
    summed = jnp.dot(
        weights_exp.astype(jnp.bfloat16), value_ref[0], preferred_element_type=jnp.float32
    )
    out_ref[0] = (summed / totals).astype(out_ref.dtype)


def attend(queries, keys_all, values_all, scale):
    spans, query_rows, channels = queries.shape
    key_rows = keys_all.shape[1]
    block = 128 if query_rows % 128 == 0 else query_rows
    kernel = lambda *refs: attend_kernel(*refs, scale=scale)
    return pl.pallas_call(
        kernel,
        grid=(spans, query_rows // block),
        in_specs=[
            pl.BlockSpec((1, block, channels), lambda f, q: (f, q, 0)),
            pl.BlockSpec((1, key_rows, channels), lambda f, q: (f, 0, 0)),
            pl.BlockSpec((1, key_rows, channels), lambda f, q: (f, 0, 0)),
        ],
        out_specs=pl.BlockSpec((1, block, channels), lambda f, q: (f, q, 0)),
        out_shape=jax.ShapeDtypeStruct(queries.shape, jnp.bfloat16),
    )(queries, keys_all, values_all)


def rms_scaled(frames, gain):
    widened = frames.astype(jnp.float32)
    mean_square = jnp.mean(widened * widened, axis=-1, keepdims=True)
    return widened * lax.rsqrt(mean_square + 1e-06) * gain


def shards(
    frames,
    earlier,
    gain_conv,
    conv_weight,
    conv_bias,
    gain_attn,
    query_weight,
    key_weight,
    value_weight,
    out_weight,
):
    span_count, row_count, col_count, channels = frames.shape
    activated = jax.nn.silu(rms_scaled(frames, gain_conv)).astype(jnp.bfloat16)
    activated = jnp.pad(activated, ((0, 0), (0, 0), (1, 1), (0, 0)))
    rimmed = padded_2(activated, (("height", 1),), 1)
    ways = lax.axis_size("tm")
    mine = lax.axis_index("tm")
    pieces = [rimmed]
    for shift in range(1, ways):
        pieces.append(
            lax.ppermute(rimmed, "tm", [(i, (i + shift) % ways) for i in range(ways)])
        )
    pieces.append(jnp.zeros_like(rimmed[:1]))
    pool = jnp.concatenate(pieces, axis=0)
    blank = ways * span_count

    def slot(index):
        place = ((mine - index // span_count) % ways) * span_count + index % span_count
        return jnp.where(index >= 0, place, blank)

    own = jnp.arange(span_count, dtype=earlier.dtype)
    picks = jnp.stack([slot(earlier[:, 0]), slot(earlier[:, 1]), own], axis=1)
    window = jnp.take(pool, picks.reshape(-1), axis=0).reshape(
        (span_count, 3) + rimmed.shape[1:]
    )
    accum = lax.conv_general_dilated(
        window,
        conv_weight,
        window_strides=(1, 1, 1),
        padding="VALID",
        dimension_numbers=("NDHWC", "DHWIO", "NDHWC"),
        preferred_element_type=jnp.float32,
    )[:, 0]
    mixed = (frames.astype(jnp.float32) + accum + conv_bias).astype(jnp.bfloat16)
    normed = rms_scaled(mixed, gain_attn).astype(jnp.bfloat16)
    tokens = normed.reshape(span_count, row_count * col_count, channels)
    queries = jnp.einsum(
        "ftc,cd->ftd", tokens, query_weight, preferred_element_type=jnp.float32
    ).astype(jnp.bfloat16)
    score_scale = 1.0 / channels**0.5
    tokens_all = ring_gather(tokens, "height", 1)
    keys_all = jnp.einsum(
        "ftc,cd->ftd", tokens_all, key_weight, preferred_element_type=jnp.float32
    ).astype(jnp.bfloat16)
    values_all = jnp.einsum(
        "ftc,cd->ftd", tokens_all, value_weight, preferred_element_type=jnp.float32
    ).astype(jnp.bfloat16)
    attended = attend(queries, keys_all, values_all, score_scale)
    projected = jnp.einsum("ftc,cd->ftd", attended, out_weight, preferred_element_type=jnp.float32)
    encoded = mixed.astype(jnp.float32) + projected.reshape(
        span_count, row_count, col_count, channels
    )
    return encoded.astype(jnp.bfloat16)


def solution(mesh):
    in_specs = (
        P(("group", "tm"), "height", None, None),
        P(("group", "tm"), None),
        P(),
        P(),
        P(),
        P(),
        P(),
        P(),
        P(),
        P(),
    )
    out_specs = P(("group", "tm"), "height", None, None)
    return jax.shard_map(shards, mesh=mesh, in_specs=in_specs, out_specs=out_specs, check_vma=False)
```

```python
import jax
import jax.numpy as jnp
from jax import lax
from jax.experimental import pallas as pl
from jax.sharding import PartitionSpec as P


def padded_2(cells, sides, width):
    for axis, dim in sides:
        count = lax.axis_size(axis)
        ends = count - 1
        head = lax.slice_in_dim(cells, 0, width, axis=dim)
        tail = lax.slice_in_dim(cells, cells.shape[dim] - width, cells.shape[dim], axis=dim)
        cells = jnp.concatenate(
            [
                lax.ppermute(tail, axis, [(i, (i + 1) % count) for i in range(ends)]),
                cells,
                lax.ppermute(head, axis, [((i + 1) % count, i) for i in range(ends)]),
            ],
            axis=dim,
        )
    return cells


def ring_gather(block, axis, dim):
    count = lax.axis_size(axis)
    ring = list(range(0, count, 2)) + list(range(count - 1 - count % 2, 0, -2))
    ahead = [(ring[p], ring[(p + 1) % count]) for p in range(count)]
    behind = [(ring[p], ring[(p - 1) % count]) for p in range(count)]
    pieces = [block]
    forward = block
    backward = block
    for step in range((count - 1) // 2):
        forward = lax.ppermute(forward, axis, ahead)
        backward = lax.ppermute(backward, axis, behind)
        pieces += [forward, backward]
    if count % 2 == 0 and count > 1:
        half = block.shape[dim] // 2
        front = lax.ppermute(lax.slice_in_dim(forward, 0, half, axis=dim), axis, ahead)
        back = lax.ppermute(
            lax.slice_in_dim(backward, half, block.shape[dim], axis=dim), axis, behind
        )
        pieces += [front, back]
    return pieces


def update_kernel(*refs, scale, first):
    if first:
        piece_ref, query_ref, key_w_ref, value_w_ref, peak_out, total_out, acc_out = refs
    else:
        (piece_ref, query_ref, key_w_ref, value_w_ref, peak_ref, total_ref, acc_ref,
         peak_out, total_out, acc_out) = refs
    piece = piece_ref[0]
    keys = jnp.dot(piece, key_w_ref[...], preferred_element_type=jnp.float32).astype(
        jnp.bfloat16
    )
    values = jnp.dot(piece, value_w_ref[...], preferred_element_type=jnp.float32).astype(
        jnp.bfloat16
    )
    scores = (
        lax.dot_general(
            query_ref[0], keys, (((1,), (1,)), ((), ())), preferred_element_type=jnp.float32
        )
        * scale
    )
    peak = jnp.max(scores, axis=-1, keepdims=True)
    if not first:
        peak = jnp.maximum(peak_ref[0], peak)
    weights_exp = jnp.exp(scores - peak)
    total = jnp.sum(weights_exp, axis=-1, keepdims=True)
    summed = jnp.dot(weights_exp.astype(jnp.bfloat16), values, preferred_element_type=jnp.float32)
    if not first:
        rescale = jnp.exp(peak_ref[0] - peak)
        total = total + total_ref[0] * rescale
        summed = summed + acc_ref[0] * rescale
    peak_out[0] = peak
    total_out[0] = total
    acc_out[0] = summed


def attend_update(piece, queries, key_weight, value_weight, state, scale):
    spans, query_rows, channels = queries.shape
    piece_rows = piece.shape[1]
    first = state is None
    kernel = lambda *refs: update_kernel(*refs, scale=scale, first=first)
    stat_spec = pl.BlockSpec((1, query_rows, 1), lambda f: (f, 0, 0))
    acc_spec = pl.BlockSpec((1, query_rows, channels), lambda f: (f, 0, 0))
    weight_spec = pl.BlockSpec((channels, channels), lambda f: (0, 0))
    in_specs = [
        pl.BlockSpec((1, piece_rows, channels), lambda f: (f, 0, 0)),
        pl.BlockSpec((1, query_rows, channels), lambda f: (f, 0, 0)),
        weight_spec,
        weight_spec,
    ]
    operands = [piece, queries, key_weight, value_weight]
    aliases = {}
    if not first:
        in_specs += [stat_spec, stat_spec, acc_spec]
        operands += list(state)
        aliases = {4: 0, 5: 1, 6: 2}
    stat_shape = jax.ShapeDtypeStruct((spans, query_rows, 1), jnp.float32)
    return pl.pallas_call(
        kernel,
        grid=(spans,),
        in_specs=in_specs,
        out_specs=[stat_spec, stat_spec, acc_spec],
        out_shape=[
            stat_shape,
            stat_shape,
            jax.ShapeDtypeStruct((spans, query_rows, channels), jnp.float32),
        ],
        input_output_aliases=aliases,
    )(*operands)


def rms_scaled(frames, gain):
    widened = frames.astype(jnp.float32)
    mean_square = jnp.mean(widened * widened, axis=-1, keepdims=True)
    return widened * lax.rsqrt(mean_square + 1e-06) * gain


def shards(
    frames,
    earlier,
    gain_conv,
    conv_weight,
    conv_bias,
    gain_attn,
    query_weight,
    key_weight,
    value_weight,
    out_weight,
):
    span_count, row_count, col_count, channels = frames.shape
    activated = jax.nn.silu(rms_scaled(frames, gain_conv)).astype(jnp.bfloat16)
    activated = jnp.pad(activated, ((0, 0), (0, 0), (1, 1), (0, 0)))
    rimmed = padded_2(activated, (("height", 1),), 1)
    ways = lax.axis_size("tm")
    mine = lax.axis_index("tm")
    pieces = [rimmed]
    for shift in range(1, ways):
        pieces.append(
            lax.ppermute(rimmed, "tm", [(i, (i + shift) % ways) for i in range(ways)])
        )
    pieces.append(jnp.zeros_like(rimmed[:1]))
    pool = jnp.concatenate(pieces, axis=0)
    blank = ways * span_count

    def slot(index):
        place = ((mine - index // span_count) % ways) * span_count + index % span_count
        return jnp.where(index >= 0, place, blank)

    own = jnp.arange(span_count, dtype=earlier.dtype)
    picks = jnp.stack([slot(earlier[:, 0]), slot(earlier[:, 1]), own], axis=1)
    window = jnp.take(pool, picks.reshape(-1), axis=0).reshape(
        (span_count, 3) + rimmed.shape[1:]
    )
    accum = lax.conv_general_dilated(
        window,
        conv_weight,
        window_strides=(1, 1, 1),
        padding="VALID",
        dimension_numbers=("NDHWC", "DHWIO", "NDHWC"),
        preferred_element_type=jnp.float32,
    )[:, 0]
    mixed = (frames.astype(jnp.float32) + accum + conv_bias).astype(jnp.bfloat16)
    normed = rms_scaled(mixed, gain_attn).astype(jnp.bfloat16)
    tokens = normed.reshape(span_count, row_count * col_count, channels)
    queries = jnp.einsum(
        "ftc,cd->ftd", tokens, query_weight, preferred_element_type=jnp.float32
    ).astype(jnp.bfloat16)
    score_scale = 1.0 / channels**0.5
    state = None
    for piece in ring_gather(tokens, "height", 1):
        state = attend_update(piece, queries, key_weight, value_weight, state, score_scale)
    _, totals, summed = state
    totals = totals[:, :, 0]
    attended = (summed / totals[:, :, None]).astype(jnp.bfloat16)
    projected = jnp.einsum("ftc,cd->ftd", attended, out_weight, preferred_element_type=jnp.float32)
    encoded = mixed.astype(jnp.float32) + projected.reshape(
        span_count, row_count, col_count, channels
    )
    return encoded.astype(jnp.bfloat16)


def solution(mesh):
    in_specs = (
        P(("group", "tm"), "height", None, None),
        P(("group", "tm"), None),
        P(),
        P(),
        P(),
        P(),
        P(),
        P(),
        P(),
        P(),
    )
    out_specs = P(("group", "tm"), "height", None, None)
    return jax.shard_map(shards, mesh=mesh, in_specs=in_specs, out_specs=out_specs, check_vma=False)
```

```python
import jax
import jax.numpy as jnp
from jax import lax
from jax.sharding import PartitionSpec as P


def padded_2(cells, sides, width):
    for axis, dim in sides:
        count = lax.axis_size(axis)
        ends = count - 1
        head = lax.slice_in_dim(cells, 0, width, axis=dim)
        tail = lax.slice_in_dim(cells, cells.shape[dim] - width, cells.shape[dim], axis=dim)
        cells = jnp.concatenate(
            [
                lax.ppermute(tail, axis, [(i, (i + 1) % count) for i in range(ends)]),
                cells,
                lax.ppermute(head, axis, [((i + 1) % count, i) for i in range(ends)]),
            ],
            axis=dim,
        )
    return cells


def ring_gather(block, axis, dim):
    count = lax.axis_size(axis)
    ring = list(range(0, count, 2)) + list(range(count - 1 - count % 2, 0, -2))
    ahead = [(ring[p], ring[(p + 1) % count]) for p in range(count)]
    behind = [(ring[p], ring[(p - 1) % count]) for p in range(count)]
    pieces = [block]
    forward = block
    backward = block
    for step in range((count - 1) // 2):
        forward = lax.ppermute(forward, axis, ahead)
        backward = lax.ppermute(backward, axis, behind)
        pieces += [forward, backward]
    if count % 2 == 0 and count > 1:
        half = block.shape[dim] // 2
        front = lax.ppermute(lax.slice_in_dim(forward, 0, half, axis=dim), axis, ahead)
        back = lax.ppermute(
            lax.slice_in_dim(backward, half, block.shape[dim], axis=dim), axis, behind
        )
        pieces += [front, back]
    return pieces


def rms_scaled(frames, gain):
    widened = frames.astype(jnp.float32)
    mean_square = jnp.mean(widened * widened, axis=-1, keepdims=True)
    return widened * lax.rsqrt(mean_square + 1e-06) * gain


def shards(
    frames,
    earlier,
    gain_conv,
    conv_weight,
    conv_bias,
    gain_attn,
    query_weight,
    key_weight,
    value_weight,
    out_weight,
):
    span_count, row_count, col_count, channels = frames.shape
    activated = jax.nn.silu(rms_scaled(frames, gain_conv)).astype(jnp.bfloat16)
    activated = jnp.pad(activated, ((0, 0), (0, 0), (1, 1), (0, 0)))
    rimmed = padded_2(activated, (("height", 1),), 1)
    ways = lax.axis_size("tm")
    mine = lax.axis_index("tm")
    pieces = [rimmed]
    for shift in range(1, ways):
        pieces.append(
            lax.ppermute(rimmed, "tm", [(i, (i + shift) % ways) for i in range(ways)])
        )
    pieces.append(jnp.zeros_like(rimmed[:1]))
    pool = jnp.concatenate(pieces, axis=0)
    blank = ways * span_count

    def slot(index):
        place = ((mine - index // span_count) % ways) * span_count + index % span_count
        return jnp.where(index >= 0, place, blank)

    own = jnp.arange(span_count, dtype=earlier.dtype)
    picks = jnp.stack([slot(earlier[:, 0]), slot(earlier[:, 1]), own], axis=1)
    window = jnp.take(pool, picks.reshape(-1), axis=0).reshape(
        (span_count, 3) + rimmed.shape[1:]
    )
    accum = lax.conv_general_dilated(
        window,
        conv_weight,
        window_strides=(1, 1, 1),
        padding="VALID",
        dimension_numbers=("NDHWC", "DHWIO", "NDHWC"),
        preferred_element_type=jnp.float32,
    )[:, 0]
    mixed = (frames.astype(jnp.float32) + accum + conv_bias).astype(jnp.bfloat16)
    normed = rms_scaled(mixed, gain_attn).astype(jnp.bfloat16)
    tokens = normed.reshape(span_count, row_count * col_count, channels)
    queries = jnp.einsum(
        "ftc,cd->ftd", tokens, query_weight, preferred_element_type=jnp.float32
    ).astype(jnp.bfloat16)
    score_scale = 1.0 / channels**0.5
    key_parts = []
    value_parts = []
    for piece in ring_gather(tokens, "height", 1):
        keys = jnp.einsum(
            "ftc,cd->ftd", piece, key_weight, preferred_element_type=jnp.float32
        ).astype(jnp.bfloat16)
        values = jnp.einsum(
            "ftc,cd->ftd", piece, value_weight, preferred_element_type=jnp.float32
        ).astype(jnp.bfloat16)
        keys, values = lax.optimization_barrier((keys, values))
        key_parts.append(keys)
        value_parts.append(values)
    keys_all = jnp.concatenate(key_parts, axis=1)
    values_all = jnp.concatenate(value_parts, axis=1)
    scores = (
        jnp.einsum("fqc,fkc->fqk", queries, keys_all, preferred_element_type=jnp.float32)
        * score_scale
    )
    peaks = jnp.max(scores, axis=-1, keepdims=True)
    weights_exp = jnp.exp(scores - peaks)
    totals = jnp.sum(weights_exp, axis=-1)
    summed = jnp.einsum(
        "fqk,fkc->fqc",
        weights_exp.astype(jnp.bfloat16),
        values_all,
        preferred_element_type=jnp.float32,
    )
    attended = (summed / totals[:, :, None]).astype(jnp.bfloat16)
    projected = jnp.einsum("ftc,cd->ftd", attended, out_weight, preferred_element_type=jnp.float32)
    encoded = mixed.astype(jnp.float32) + projected.reshape(
        span_count, row_count, col_count, channels
    )
    return encoded.astype(jnp.bfloat16)


def solution(mesh):
    in_specs = (
        P(("group", "tm"), "height", None, None),
        P(("group", "tm"), None),
        P(),
        P(),
        P(),
        P(),
        P(),
        P(),
        P(),
        P(),
    )
    out_specs = P(("group", "tm"), "height", None, None)
    return jax.shard_map(shards, mesh=mesh, in_specs=in_specs, out_specs=out_specs, check_vma=False)
```

```python
import jax
import jax.numpy as jnp
from jax import lax
from jax.experimental import pallas as pl
from jax.sharding import PartitionSpec as P


def padded_2(cells, sides, width):
    for axis, dim in sides:
        count = lax.axis_size(axis)
        ends = count - 1
        head = lax.slice_in_dim(cells, 0, width, axis=dim)
        tail = lax.slice_in_dim(cells, cells.shape[dim] - width, cells.shape[dim], axis=dim)
        cells = jnp.concatenate(
            [
                lax.ppermute(tail, axis, [(i, (i + 1) % count) for i in range(ends)]),
                cells,
                lax.ppermute(head, axis, [((i + 1) % count, i) for i in range(ends)]),
            ],
            axis=dim,
        )
    return cells


def ring_gather(block, axis, dim):
    count = lax.axis_size(axis)
    ring = list(range(0, count, 2)) + list(range(count - 1 - count % 2, 0, -2))
    ahead = [(ring[p], ring[(p + 1) % count]) for p in range(count)]
    behind = [(ring[p], ring[(p - 1) % count]) for p in range(count)]
    pieces = [block]
    forward = block
    backward = block
    for step in range((count - 1) // 2):
        forward = lax.ppermute(forward, axis, ahead)
        backward = lax.ppermute(backward, axis, behind)
        pieces += [forward, backward]
    if count % 2 == 0 and count > 1:
        half = block.shape[dim] // 2
        front = lax.ppermute(lax.slice_in_dim(forward, 0, half, axis=dim), axis, ahead)
        back = lax.ppermute(
            lax.slice_in_dim(backward, half, block.shape[dim], axis=dim), axis, behind
        )
        pieces += [front, back]
    return jnp.concatenate(pieces, axis=dim)


def attend_kernel(query_ref, key_ref, value_ref, out_ref, *, scale):
    scores = jnp.dot(query_ref[0], key_ref[0], preferred_element_type=jnp.float32) * scale
    peaks = jnp.max(scores, axis=-1, keepdims=True)
    weights_exp = jnp.exp(scores - peaks)
    totals = jnp.sum(weights_exp, axis=-1, keepdims=True)
    summed = jnp.dot(
        weights_exp.astype(jnp.bfloat16), value_ref[0], preferred_element_type=jnp.float32
    )
    out_ref[0] = (summed / totals).astype(out_ref.dtype)


def attend(queries, keys_all, values_all, scale):
    spans, query_rows, channels = queries.shape
    key_rows = keys_all.shape[2]
    block = query_rows
    kernel = lambda *refs: attend_kernel(*refs, scale=scale)
    return pl.pallas_call(
        kernel,
        grid=(spans, query_rows // block),
        in_specs=[
            pl.BlockSpec((1, block, channels), lambda f, q: (f, q, 0)),
            pl.BlockSpec((1, channels, key_rows), lambda f, q: (f, 0, 0)),
            pl.BlockSpec((1, key_rows, channels), lambda f, q: (f, 0, 0)),
        ],
        out_specs=pl.BlockSpec((1, block, channels), lambda f, q: (f, q, 0)),
        out_shape=jax.ShapeDtypeStruct(queries.shape, jnp.bfloat16),
    )(queries, keys_all, values_all)


def rms_scaled(frames, gain):
    widened = frames.astype(jnp.float32)
    mean_square = jnp.mean(widened * widened, axis=-1, keepdims=True)
    return widened * lax.rsqrt(mean_square + 1e-06) * gain


def shards(
    frames,
    earlier,
    gain_conv,
    conv_weight,
    conv_bias,
    gain_attn,
    query_weight,
    key_weight,
    value_weight,
    out_weight,
):
    span_count, row_count, col_count, channels = frames.shape
    activated = jax.nn.silu(rms_scaled(frames, gain_conv)).astype(jnp.bfloat16)
    activated = jnp.pad(activated, ((0, 0), (0, 0), (1, 1), (0, 0)))
    rimmed = padded_2(activated, (("height", 1),), 1)
    ways = lax.axis_size("tm")
    mine = lax.axis_index("tm")
    pieces = [rimmed]
    for shift in range(1, ways):
        pieces.append(
            lax.ppermute(rimmed, "tm", [(i, (i + shift) % ways) for i in range(ways)])
        )
    pieces.append(jnp.zeros_like(rimmed[:1]))
    pool = jnp.concatenate(pieces, axis=0)
    blank = ways * span_count

    def slot(index):
        place = ((mine - index // span_count) % ways) * span_count + index % span_count
        return jnp.where(index >= 0, place, blank)

    own = jnp.arange(span_count, dtype=earlier.dtype)
    picks = jnp.stack([slot(earlier[:, 0]), slot(earlier[:, 1]), own], axis=1)
    window = jnp.take(pool, picks.reshape(-1), axis=0).reshape(
        (span_count, 3) + rimmed.shape[1:]
    )
    accum = lax.conv_general_dilated(
        window,
        conv_weight,
        window_strides=(1, 1, 1),
        padding="VALID",
        dimension_numbers=("NDHWC", "DHWIO", "NDHWC"),
        preferred_element_type=jnp.float32,
    )[:, 0]
    mixed = (frames.astype(jnp.float32) + accum + conv_bias).astype(jnp.bfloat16)
    normed = rms_scaled(mixed, gain_attn).astype(jnp.bfloat16)
    tokens = normed.reshape(span_count, row_count * col_count, channels)
    queries = jnp.einsum(
        "ftc,cd->ftd", tokens, query_weight, preferred_element_type=jnp.float32
    ).astype(jnp.bfloat16)
    score_scale = 1.0 / channels**0.5
    tokens_all = ring_gather(tokens, "height", 1)
    keys_all = jnp.einsum(
        "ftc,cd->fdt", tokens_all, key_weight, preferred_element_type=jnp.float32
    ).astype(jnp.bfloat16)
    values_all = jnp.einsum(
        "ftc,cd->ftd", tokens_all, value_weight, preferred_element_type=jnp.float32
    ).astype(jnp.bfloat16)
    attended = attend(queries, keys_all, values_all, score_scale)
    projected = jnp.einsum("ftc,cd->ftd", attended, out_weight, preferred_element_type=jnp.float32)
    encoded = mixed.astype(jnp.float32) + projected.reshape(
        span_count, row_count, col_count, channels
    )
    return encoded.astype(jnp.bfloat16)


def solution(mesh):
    in_specs = (
        P(("group", "tm"), "height", None, None),
        P(("group", "tm"), None),
        P(),
        P(),
        P(),
        P(),
        P(),
        P(),
        P(),
        P(),
    )
    out_specs = P(("group", "tm"), "height", None, None)
    return jax.shard_map(shards, mesh=mesh, in_specs=in_specs, out_specs=out_specs, check_vma=False)
```

```python
import jax
import jax.numpy as jnp
from jax import lax
from jax.experimental import pallas as pl
from jax.sharding import PartitionSpec as P


def padded_2(cells, sides, width):
    for axis, dim in sides:
        count = lax.axis_size(axis)
        ends = count - 1
        head = lax.slice_in_dim(cells, 0, width, axis=dim)
        tail = lax.slice_in_dim(cells, cells.shape[dim] - width, cells.shape[dim], axis=dim)
        cells = jnp.concatenate(
            [
                lax.ppermute(tail, axis, [(i, (i + 1) % count) for i in range(ends)]),
                cells,
                lax.ppermute(head, axis, [((i + 1) % count, i) for i in range(ends)]),
            ],
            axis=dim,
        )
    return cells


def ring_gather(block, axis, dim):
    count = lax.axis_size(axis)
    ring = list(range(0, count, 2)) + list(range(count - 1 - count % 2, 0, -2))
    ahead = [(ring[p], ring[(p + 1) % count]) for p in range(count)]
    behind = [(ring[p], ring[(p - 1) % count]) for p in range(count)]
    pieces = [block]
    forward = block
    backward = block
    for step in range((count - 1) // 2):
        forward = lax.ppermute(forward, axis, ahead)
        backward = lax.ppermute(backward, axis, behind)
        pieces += [forward, backward]
    if count % 2 == 0 and count > 1:
        half = block.shape[dim] // 2
        front = lax.ppermute(lax.slice_in_dim(forward, 0, half, axis=dim), axis, ahead)
        back = lax.ppermute(
            lax.slice_in_dim(backward, half, block.shape[dim], axis=dim), axis, behind
        )
        pieces += [front, back]
    return jnp.concatenate(pieces, axis=dim)


def attend_kernel(query_ref, token_ref, key_w_ref, value_w_ref, out_ref, *, scale):
    tokens = token_ref[0]
    keys = jnp.dot(tokens, key_w_ref[...], preferred_element_type=jnp.float32).astype(
        jnp.bfloat16
    )
    values = jnp.dot(tokens, value_w_ref[...], preferred_element_type=jnp.float32).astype(
        jnp.bfloat16
    )
    scores = (
        lax.dot_general(
            query_ref[0], keys, (((1,), (1,)), ((), ())), preferred_element_type=jnp.float32
        )
        * scale
    )
    peaks = jnp.max(scores, axis=-1, keepdims=True)
    weights_exp = jnp.exp(scores - peaks)
    totals = jnp.sum(weights_exp, axis=-1, keepdims=True)
    summed = jnp.dot(weights_exp.astype(jnp.bfloat16), values, preferred_element_type=jnp.float32)
    out_ref[0] = (summed / totals).astype(out_ref.dtype)


def attend(queries, tokens_all, key_weight, value_weight, scale):
    spans, query_rows, channels = queries.shape
    key_rows = tokens_all.shape[1]
    kernel = lambda *refs: attend_kernel(*refs, scale=scale)
    weight_spec = pl.BlockSpec((channels, channels), lambda f: (0, 0))
    return pl.pallas_call(
        kernel,
        grid=(spans,),
        in_specs=[
            pl.BlockSpec((1, query_rows, channels), lambda f: (f, 0, 0)),
            pl.BlockSpec((1, key_rows, channels), lambda f: (f, 0, 0)),
            weight_spec,
            weight_spec,
        ],
        out_specs=pl.BlockSpec((1, query_rows, channels), lambda f: (f, 0, 0)),
        out_shape=jax.ShapeDtypeStruct(queries.shape, jnp.bfloat16),
    )(queries, tokens_all, key_weight, value_weight)


def rms_scaled(frames, gain):
    widened = frames.astype(jnp.float32)
    mean_square = jnp.mean(widened * widened, axis=-1, keepdims=True)
    return widened * lax.rsqrt(mean_square + 1e-06) * gain


def shards(
    frames,
    earlier,
    gain_conv,
    conv_weight,
    conv_bias,
    gain_attn,
    query_weight,
    key_weight,
    value_weight,
    out_weight,
):
    span_count, row_count, col_count, channels = frames.shape
    activated = jax.nn.silu(rms_scaled(frames, gain_conv)).astype(jnp.bfloat16)
    activated = jnp.pad(activated, ((0, 0), (0, 0), (1, 1), (0, 0)))
    rimmed = padded_2(activated, (("height", 1),), 1)
    ways = lax.axis_size("tm")
    mine = lax.axis_index("tm")
    pieces = [rimmed]
    for shift in range(1, ways):
        pieces.append(
            lax.ppermute(rimmed, "tm", [(i, (i + shift) % ways) for i in range(ways)])
        )
    pieces.append(jnp.zeros_like(rimmed[:1]))
    pool = jnp.concatenate(pieces, axis=0)
    blank = ways * span_count

    def slot(index):
        place = ((mine - index // span_count) % ways) * span_count + index % span_count
        return jnp.where(index >= 0, place, blank)

    own = jnp.arange(span_count, dtype=earlier.dtype)
    picks = jnp.stack([slot(earlier[:, 0]), slot(earlier[:, 1]), own], axis=1)
    window = jnp.take(pool, picks.reshape(-1), axis=0).reshape(
        (span_count, 3) + rimmed.shape[1:]
    )
    accum = lax.conv_general_dilated(
        window,
        conv_weight,
        window_strides=(1, 1, 1),
        padding="VALID",
        dimension_numbers=("NDHWC", "DHWIO", "NDHWC"),
        preferred_element_type=jnp.float32,
    )[:, 0]
    mixed = (frames.astype(jnp.float32) + accum + conv_bias).astype(jnp.bfloat16)
    normed = rms_scaled(mixed, gain_attn).astype(jnp.bfloat16)
    tokens = normed.reshape(span_count, row_count * col_count, channels)
    queries = jnp.einsum(
        "ftc,cd->ftd", tokens, query_weight, preferred_element_type=jnp.float32
    ).astype(jnp.bfloat16)
    score_scale = 1.0 / channels**0.5
    tokens_all = ring_gather(tokens, "height", 1)
    attended = attend(queries, tokens_all, key_weight, value_weight, score_scale)
    projected = jnp.einsum("ftc,cd->ftd", attended, out_weight, preferred_element_type=jnp.float32)
    encoded = mixed.astype(jnp.float32) + projected.reshape(
        span_count, row_count, col_count, channels
    )
    return encoded.astype(jnp.bfloat16)


def solution(mesh):
    in_specs = (
        P(("group", "tm"), "height", None, None),
        P(("group", "tm"), None),
        P(),
        P(),
        P(),
        P(),
        P(),
        P(),
        P(),
        P(),
    )
    out_specs = P(("group", "tm"), "height", None, None)
    return jax.shard_map(shards, mesh=mesh, in_specs=in_specs, out_specs=out_specs, check_vma=False)
```

```python
import jax
import jax.numpy as jnp
from jax import lax
from jax.sharding import PartitionSpec as P


def padded_2(cells, sides, width):
    for axis, dim in sides:
        count = lax.axis_size(axis)
        ends = count - 1
        head = lax.slice_in_dim(cells, 0, width, axis=dim)
        tail = lax.slice_in_dim(cells, cells.shape[dim] - width, cells.shape[dim], axis=dim)
        cells = jnp.concatenate(
            [
                lax.ppermute(tail, axis, [(i, (i + 1) % count) for i in range(ends)]),
                cells,
                lax.ppermute(head, axis, [((i + 1) % count, i) for i in range(ends)]),
            ],
            axis=dim,
        )
    return cells


def ring_gather(block, axis, dim):
    count = lax.axis_size(axis)
    ring = list(range(0, count, 2)) + list(range(count - 1 - count % 2, 0, -2))
    ahead = [(ring[p], ring[(p + 1) % count]) for p in range(count)]
    behind = [(ring[p], ring[(p - 1) % count]) for p in range(count)]
    pieces = [block]
    forward = block
    backward = block
    for step in range((count - 1) // 2):
        forward = lax.ppermute(forward, axis, ahead)
        backward = lax.ppermute(backward, axis, behind)
        pieces += [forward, backward]
    if count % 2 == 0 and count > 1:
        half = block.shape[dim] // 2
        front = lax.ppermute(lax.slice_in_dim(forward, 0, half, axis=dim), axis, ahead)
        back = lax.ppermute(
            lax.slice_in_dim(backward, half, block.shape[dim], axis=dim), axis, behind
        )
        pieces += [front, back]
    return jnp.concatenate(pieces, axis=dim)


def rms_scaled(frames, gain):
    widened = frames.astype(jnp.float32)
    mean_square = jnp.mean(widened * widened, axis=-1, keepdims=True)
    return widened * lax.rsqrt(mean_square + 1e-06) * gain


def shards(
    frames,
    earlier,
    gain_conv,
    conv_weight,
    conv_bias,
    gain_attn,
    query_weight,
    key_weight,
    value_weight,
    out_weight,
):
    span_count, row_count, col_count, channels = frames.shape
    activated = jax.nn.silu(rms_scaled(frames, gain_conv)).astype(jnp.bfloat16)
    activated = jnp.pad(activated, ((0, 0), (0, 0), (1, 1), (0, 0)))
    heights = lax.axis_size("height")
    last = heights - 1
    top = lax.ppermute(activated[:, -1:], "height", [(i, i + 1) for i in range(last)])
    bottom = lax.ppermute(activated[:, :1], "height", [(i + 1, i) for i in range(last)])
    ways = lax.axis_size("tm")
    mine = lax.axis_index("tm")
    blank = ways * span_count

    def pooled(block):
        pieces = [block]
        for shift in range(1, ways):
            pieces.append(
                lax.ppermute(block, "tm", [(i, (i + shift) % ways) for i in range(ways)])
            )
        pieces.append(jnp.zeros_like(block[:1]))
        return jnp.concatenate(pieces, axis=0)

    def slot(index):
        place = ((mine - index // span_count) % ways) * span_count + index % span_count
        return jnp.where(index >= 0, place, blank)

    own = jnp.arange(span_count, dtype=earlier.dtype)
    picks = jnp.stack([slot(earlier[:, 0]), slot(earlier[:, 1]), own], axis=1).reshape(-1)

    def windowed(block):
        taken = jnp.take(pooled(block), picks, axis=0)
        return taken.reshape((span_count, 3) + block.shape[1:])

    def conv(window, weight):
        return lax.conv_general_dilated(
            window,
            weight,
            window_strides=(1, 1, 1),
            padding="VALID",
            dimension_numbers=("NDHWC", "DHWIO", "NDHWC"),
            preferred_element_type=jnp.float32,
        )[:, 0]

    core = conv(
        jnp.pad(windowed(activated), ((0, 0), (0, 0), (1, 1), (0, 0), (0, 0))), conv_weight
    )
    core, top, bottom = lax.optimization_barrier((core, top, bottom))
    rims = windowed(jnp.concatenate([top, bottom], axis=1))
    upper = conv(rims[:, :, :1], conv_weight[:, :1])
    lower = conv(rims[:, :, 1:], conv_weight[:, 2:])
    edges = jnp.concatenate(
        [upper, jnp.zeros_like(core[:, : row_count - 2]), lower], axis=1
    )
    accum = core + edges
    mixed = (frames.astype(jnp.float32) + accum + conv_bias).astype(jnp.bfloat16)
    normed = rms_scaled(mixed, gain_attn).astype(jnp.bfloat16)
    tokens = normed.reshape(span_count, row_count * col_count, channels)
    queries = jnp.einsum(
        "ftc,cd->ftd", tokens, query_weight, preferred_element_type=jnp.float32
    ).astype(jnp.bfloat16)
    score_scale = 1.0 / channels**0.5
    tokens_all = ring_gather(tokens, "height", 1)
    keys_all = jnp.einsum(
        "ftc,cd->ftd", tokens_all, key_weight, preferred_element_type=jnp.float32
    ).astype(jnp.bfloat16)
    values_all = jnp.einsum(
        "ftc,cd->ftd", tokens_all, value_weight, preferred_element_type=jnp.float32
    ).astype(jnp.bfloat16)
    scores = (
        jnp.einsum("fqc,fkc->fqk", queries, keys_all, preferred_element_type=jnp.float32)
        * score_scale
    )
    peaks = jnp.max(scores, axis=-1, keepdims=True)
    weights_exp = jnp.exp(scores - peaks)
    totals = jnp.sum(weights_exp, axis=-1)
    summed = jnp.einsum(
        "fqk,fkc->fqc",
        weights_exp.astype(jnp.bfloat16),
        values_all,
        preferred_element_type=jnp.float32,
    )
    attended = (summed / totals[:, :, None]).astype(jnp.bfloat16)
    projected = jnp.einsum("ftc,cd->ftd", attended, out_weight, preferred_element_type=jnp.float32)
    encoded = mixed.astype(jnp.float32) + projected.reshape(
        span_count, row_count, col_count, channels
    )
    return encoded.astype(jnp.bfloat16)


def solution(mesh):
    in_specs = (
        P(("group", "tm"), "height", None, None),
        P(("group", "tm"), None),
        P(),
        P(),
        P(),
        P(),
        P(),
        P(),
        P(),
        P(),
    )
    out_specs = P(("group", "tm"), "height", None, None)
    return jax.shard_map(shards, mesh=mesh, in_specs=in_specs, out_specs=out_specs, check_vma=False)
```

```python
import jax
import jax.numpy as jnp
from jax import lax
from jax.sharding import PartitionSpec as P


def padded_2(cells, sides, width):
    for axis, dim in sides:
        count = lax.axis_size(axis)
        ends = count - 1
        head = lax.slice_in_dim(cells, 0, width, axis=dim)
        tail = lax.slice_in_dim(cells, cells.shape[dim] - width, cells.shape[dim], axis=dim)
        cells = jnp.concatenate(
            [
                lax.ppermute(tail, axis, [(i, (i + 1) % count) for i in range(ends)]),
                cells,
                lax.ppermute(head, axis, [((i + 1) % count, i) for i in range(ends)]),
            ],
            axis=dim,
        )
    return cells


def ring_gather(block, axis, dim):
    count = lax.axis_size(axis)
    ring = list(range(0, count, 2)) + list(range(count - 1 - count % 2, 0, -2))
    ahead = [(ring[p], ring[(p + 1) % count]) for p in range(count)]
    behind = [(ring[p], ring[(p - 1) % count]) for p in range(count)]
    pieces = [block]
    forward = block
    backward = block
    for step in range((count - 1) // 2):
        forward = lax.ppermute(forward, axis, ahead)
        backward = lax.ppermute(backward, axis, behind)
        pieces += [forward, backward]
    if count % 2 == 0 and count > 1:
        half = block.shape[dim] // 2
        front = lax.ppermute(lax.slice_in_dim(forward, 0, half, axis=dim), axis, ahead)
        back = lax.ppermute(
            lax.slice_in_dim(backward, half, block.shape[dim], axis=dim), axis, behind
        )
        pieces += [front, back]
    return jnp.concatenate(pieces, axis=dim)


def rms_scaled(frames, gain):
    widened = frames.astype(jnp.float32)
    mean_square = jnp.mean(widened * widened, axis=-1, keepdims=True)
    return widened * lax.rsqrt(mean_square + 1e-06) * gain


def shards(
    frames,
    earlier,
    gain_conv,
    conv_weight,
    conv_bias,
    gain_attn,
    query_weight,
    key_weight,
    value_weight,
    out_weight,
):
    span_count, row_count, col_count, channels = frames.shape
    rims = padded_2(frames, (("height", 1),), 1)
    rims = jnp.concatenate([rims[:, :1], rims[:, -1:]], axis=1)
    activated = jax.nn.silu(rms_scaled(frames, gain_conv)).astype(jnp.bfloat16)
    rims = jax.nn.silu(rms_scaled(rims, gain_conv)).astype(jnp.bfloat16)
    rimmed = jnp.concatenate([rims[:, :1], activated, rims[:, 1:]], axis=1)
    rimmed = jnp.pad(rimmed, ((0, 0), (0, 0), (1, 1), (0, 0)))
    ways = lax.axis_size("tm")
    mine = lax.axis_index("tm")
    pieces = [rimmed]
    for shift in range(1, ways):
        pieces.append(
            lax.ppermute(rimmed, "tm", [(i, (i + shift) % ways) for i in range(ways)])
        )
    pieces.append(jnp.zeros_like(rimmed[:1]))
    pool = jnp.concatenate(pieces, axis=0)
    blank = ways * span_count

    def slot(index):
        place = ((mine - index // span_count) % ways) * span_count + index % span_count
        return jnp.where(index >= 0, place, blank)

    own = jnp.arange(span_count, dtype=earlier.dtype)
    picks = jnp.stack([slot(earlier[:, 0]), slot(earlier[:, 1]), own], axis=1)
    window = jnp.take(pool, picks.reshape(-1), axis=0).reshape(
        (span_count, 3) + rimmed.shape[1:]
    )
    accum = lax.conv_general_dilated(
        window,
        conv_weight,
        window_strides=(1, 1, 1),
        padding="VALID",
        dimension_numbers=("NDHWC", "DHWIO", "NDHWC"),
        preferred_element_type=jnp.float32,
    )[:, 0]
    mixed = (frames.astype(jnp.float32) + accum + conv_bias).astype(jnp.bfloat16)
    normed = rms_scaled(mixed, gain_attn).astype(jnp.bfloat16)
    tokens = normed.reshape(span_count, row_count * col_count, channels)
    queries = jnp.einsum(
        "ftc,cd->ftd", tokens, query_weight, preferred_element_type=jnp.float32
    ).astype(jnp.bfloat16)
    score_scale = 1.0 / channels**0.5
    tokens_all = ring_gather(tokens, "height", 1)
    keys_all = jnp.einsum(
        "ftc,cd->ftd", tokens_all, key_weight, preferred_element_type=jnp.float32
    ).astype(jnp.bfloat16)
    values_all = jnp.einsum(
        "ftc,cd->ftd", tokens_all, value_weight, preferred_element_type=jnp.float32
    ).astype(jnp.bfloat16)
    scores = (
        jnp.einsum("fqc,fkc->fqk", queries, keys_all, preferred_element_type=jnp.float32)
        * score_scale
    )
    peaks = jnp.max(scores, axis=-1, keepdims=True)
    weights_exp = jnp.exp(scores - peaks)
    totals = jnp.sum(weights_exp, axis=-1)
    summed = jnp.einsum(
        "fqk,fkc->fqc",
        weights_exp.astype(jnp.bfloat16),
        values_all,
        preferred_element_type=jnp.float32,
    )
    attended = (summed / totals[:, :, None]).astype(jnp.bfloat16)
    projected = jnp.einsum("ftc,cd->ftd", attended, out_weight, preferred_element_type=jnp.float32)
    encoded = mixed.astype(jnp.float32) + projected.reshape(
        span_count, row_count, col_count, channels
    )
    return encoded.astype(jnp.bfloat16)


def solution(mesh):
    in_specs = (
        P(("group", "tm"), "height", None, None),
        P(("group", "tm"), None),
        P(),
        P(),
        P(),
        P(),
        P(),
        P(),
        P(),
        P(),
    )
    out_specs = P(("group", "tm"), "height", None, None)
    return jax.shard_map(shards, mesh=mesh, in_specs=in_specs, out_specs=out_specs, check_vma=False)
```

```python
import jax
import jax.numpy as jnp
from jax import lax
from jax.sharding import PartitionSpec as P


def padded_2(cells, sides, width):
    for axis, dim in sides:
        count = lax.axis_size(axis)
        ends = count - 1
        head = lax.slice_in_dim(cells, 0, width, axis=dim)
        tail = lax.slice_in_dim(cells, cells.shape[dim] - width, cells.shape[dim], axis=dim)
        cells = jnp.concatenate(
            [
                lax.ppermute(tail, axis, [(i, (i + 1) % count) for i in range(ends)]),
                cells,
                lax.ppermute(head, axis, [((i + 1) % count, i) for i in range(ends)]),
            ],
            axis=dim,
        )
    return cells


def ring_gather(block, axis, dim):
    count = lax.axis_size(axis)
    ring = list(range(0, count, 2)) + list(range(count - 1 - count % 2, 0, -2))
    ahead = [(ring[p], ring[(p + 1) % count]) for p in range(count)]
    behind = [(ring[p], ring[(p - 1) % count]) for p in range(count)]
    pieces = [block]
    forward = block
    backward = block
    for step in range((count - 1) // 2):
        forward = lax.ppermute(forward, axis, ahead)
        backward = lax.ppermute(backward, axis, behind)
        pieces += [forward, backward]
    if count % 2 == 0 and count > 1:
        half = block.shape[dim] // 2
        front = lax.ppermute(lax.slice_in_dim(forward, 0, half, axis=dim), axis, ahead)
        back = lax.ppermute(
            lax.slice_in_dim(backward, half, block.shape[dim], axis=dim), axis, behind
        )
        pieces += [front, back]
    return pieces


def rms_scaled(frames, gain):
    widened = frames.astype(jnp.float32)
    mean_square = jnp.mean(widened * widened, axis=-1, keepdims=True)
    return widened * lax.rsqrt(mean_square + 1e-06) * gain


def shards(
    frames,
    earlier,
    gain_conv,
    conv_weight,
    conv_bias,
    gain_attn,
    query_weight,
    key_weight,
    value_weight,
    out_weight,
):
    span_count, row_count, col_count, channels = frames.shape
    rims = padded_2(frames, (("height", 1),), 1)
    rims = jnp.concatenate([rims[:, :1], rims[:, -1:]], axis=1)
    activated = jax.nn.silu(rms_scaled(frames, gain_conv)).astype(jnp.bfloat16)
    rims = jax.nn.silu(rms_scaled(rims, gain_conv)).astype(jnp.bfloat16)
    rimmed = jnp.concatenate([rims[:, :1], activated, rims[:, 1:]], axis=1)
    rimmed = jnp.pad(rimmed, ((0, 0), (0, 0), (1, 1), (0, 0)))
    ways = lax.axis_size("tm")
    mine = lax.axis_index("tm")
    pieces = [rimmed]
    for shift in range(1, ways):
        pieces.append(
            lax.ppermute(rimmed, "tm", [(i, (i + shift) % ways) for i in range(ways)])
        )
    pieces.append(jnp.zeros_like(rimmed[:1]))
    pool = jnp.concatenate(pieces, axis=0)
    blank = ways * span_count

    def slot(index):
        place = ((mine - index // span_count) % ways) * span_count + index % span_count
        return jnp.where(index >= 0, place, blank)

    own = jnp.arange(span_count, dtype=earlier.dtype)
    picks = jnp.stack([slot(earlier[:, 0]), slot(earlier[:, 1]), own], axis=1)
    window = jnp.take(pool, picks.reshape(-1), axis=0).reshape(
        (span_count, 3) + rimmed.shape[1:]
    )
    score_scale = 1.0 / channels**0.5
    outputs = []
    span_window = window[:1]
    for span in range(span_count):
        accum = lax.conv_general_dilated(
            span_window,
            conv_weight,
            window_strides=(1, 1, 1),
            padding="VALID",
            dimension_numbers=("NDHWC", "DHWIO", "NDHWC"),
            preferred_element_type=jnp.float32,
        )[:, 0]
        mixed = (frames[span : span + 1].astype(jnp.float32) + accum + conv_bias).astype(
            jnp.bfloat16
        )
        normed = rms_scaled(mixed, gain_attn).astype(jnp.bfloat16)
        tokens = normed.reshape(1, row_count * col_count, channels)
        queries = jnp.einsum(
            "ftc,cd->ftd", tokens, query_weight, preferred_element_type=jnp.float32
        ).astype(jnp.bfloat16)
        pieces = ring_gather(tokens, "height", 1)
        if span + 1 < span_count:
            pieces[1], span_window = lax.optimization_barrier(
                (pieces[1], window[span + 1 : span + 2])
            )
        tokens_all = jnp.concatenate(pieces, axis=1)
        keys_all = jnp.einsum(
            "ftc,cd->ftd", tokens_all, key_weight, preferred_element_type=jnp.float32
        ).astype(jnp.bfloat16)
        values_all = jnp.einsum(
            "ftc,cd->ftd", tokens_all, value_weight, preferred_element_type=jnp.float32
        ).astype(jnp.bfloat16)
        scores = (
            jnp.einsum("fqc,fkc->fqk", queries, keys_all, preferred_element_type=jnp.float32)
            * score_scale
        )
        peaks = jnp.max(scores, axis=-1, keepdims=True)
        weights_exp = jnp.exp(scores - peaks)
        totals = jnp.sum(weights_exp, axis=-1)
        summed = jnp.einsum(
            "fqk,fkc->fqc",
            weights_exp.astype(jnp.bfloat16),
            values_all,
            preferred_element_type=jnp.float32,
        )
        attended = (summed / totals[:, :, None]).astype(jnp.bfloat16)
        projected = jnp.einsum(
            "ftc,cd->ftd", attended, out_weight, preferred_element_type=jnp.float32
        )
        encoded = mixed.astype(jnp.float32) + projected.reshape(mixed.shape)
        outputs.append(encoded.astype(jnp.bfloat16))
    return jnp.concatenate(outputs, axis=0)


def solution(mesh):
    in_specs = (
        P(("group", "tm"), "height", None, None),
        P(("group", "tm"), None),
        P(),
        P(),
        P(),
        P(),
        P(),
        P(),
        P(),
        P(),
    )
    out_specs = P(("group", "tm"), "height", None, None)
    return jax.shard_map(shards, mesh=mesh, in_specs=in_specs, out_specs=out_specs, check_vma=False)
```

```python
import jax
import jax.numpy as jnp
from jax import lax
from jax.sharding import PartitionSpec as P


def padded_2(cells, sides, width):
    for axis, dim in sides:
        count = lax.axis_size(axis)
        ends = count - 1
        head = lax.slice_in_dim(cells, 0, width, axis=dim)
        tail = lax.slice_in_dim(cells, cells.shape[dim] - width, cells.shape[dim], axis=dim)
        cells = jnp.concatenate(
            [
                lax.ppermute(tail, axis, [(i, (i + 1) % count) for i in range(ends)]),
                cells,
                lax.ppermute(head, axis, [((i + 1) % count, i) for i in range(ends)]),
            ],
            axis=dim,
        )
    return cells


def ring_gather(block, axis, dim):
    count = lax.axis_size(axis)
    ring = list(range(0, count, 2)) + list(range(count - 1 - count % 2, 0, -2))
    ahead = [(ring[p], ring[(p + 1) % count]) for p in range(count)]
    behind = [(ring[p], ring[(p - 1) % count]) for p in range(count)]
    pieces = [block]
    forward = block
    backward = block
    for step in range((count - 1) // 2):
        forward = lax.ppermute(forward, axis, ahead)
        backward = lax.ppermute(backward, axis, behind)
        pieces += [forward, backward]
    if count % 2 == 0 and count > 1:
        half = block.shape[dim] // 2
        front = lax.ppermute(lax.slice_in_dim(forward, 0, half, axis=dim), axis, ahead)
        back = lax.ppermute(
            lax.slice_in_dim(backward, half, block.shape[dim], axis=dim), axis, behind
        )
        pieces += [front, back]
    return pieces


def rms_scaled(frames, gain):
    widened = frames.astype(jnp.float32)
    mean_square = jnp.mean(widened * widened, axis=-1, keepdims=True)
    return widened * lax.rsqrt(mean_square + 1e-06) * gain


def shards(
    frames,
    earlier,
    gain_conv,
    conv_weight,
    conv_bias,
    gain_attn,
    query_weight,
    key_weight,
    value_weight,
    out_weight,
):
    span_count, row_count, col_count, channels = frames.shape
    rims = padded_2(frames, (("height", 1),), 1)
    rims = jnp.concatenate([rims[:, :1], rims[:, -1:]], axis=1)
    activated = jax.nn.silu(rms_scaled(frames, gain_conv)).astype(jnp.bfloat16)
    rims = jax.nn.silu(rms_scaled(rims, gain_conv)).astype(jnp.bfloat16)
    rimmed = jnp.concatenate([rims[:, :1], activated, rims[:, 1:]], axis=1)
    rimmed = jnp.pad(rimmed, ((0, 0), (0, 0), (1, 1), (0, 0)))
    ways = lax.axis_size("tm")
    mine = lax.axis_index("tm")
    pieces = [rimmed]
    for shift in range(1, ways):
        pieces.append(
            lax.ppermute(rimmed, "tm", [(i, (i + shift) % ways) for i in range(ways)])
        )
    pieces.append(jnp.zeros_like(rimmed[:1]))
    pool = jnp.concatenate(pieces, axis=0)
    blank = ways * span_count

    def slot(index):
        place = ((mine - index // span_count) % ways) * span_count + index % span_count
        return jnp.where(index >= 0, place, blank)

    own = jnp.arange(span_count, dtype=earlier.dtype)
    picks = jnp.stack([slot(earlier[:, 0]), slot(earlier[:, 1]), own], axis=1)
    window = jnp.take(pool, picks.reshape(-1), axis=0, mode="clip").reshape(
        (span_count, 3) + rimmed.shape[1:]
    )
    score_scale = 1.0 / channels**0.5
    outputs = []
    span_window = window[:1]
    for span in range(span_count):
        accum = lax.conv_general_dilated(
            span_window,
            conv_weight,
            window_strides=(1, 1, 1),
            padding="VALID",
            dimension_numbers=("NDHWC", "DHWIO", "NDHWC"),
            preferred_element_type=jnp.float32,
        )[:, 0]
        mixed = (frames[span : span + 1].astype(jnp.float32) + accum + conv_bias).astype(
            jnp.bfloat16
        )
        normed = rms_scaled(mixed, gain_attn).astype(jnp.bfloat16)
        tokens = normed.reshape(1, row_count * col_count, channels)
        queries = jnp.einsum(
            "ftc,cd->ftd", tokens, query_weight, preferred_element_type=jnp.float32
        ).astype(jnp.bfloat16)
        pieces = ring_gather(tokens, "height", 1)
        if span + 1 < span_count:
            pieces[1], span_window = lax.optimization_barrier(
                (pieces[1], window[span + 1 : span + 2])
            )
        tokens_all = jnp.concatenate(pieces, axis=1)
        keys_all = jnp.einsum(
            "ftc,cd->ftd", tokens_all, key_weight, preferred_element_type=jnp.float32
        ).astype(jnp.bfloat16)
        values_all = jnp.einsum(
            "ftc,cd->ftd", tokens_all, value_weight, preferred_element_type=jnp.float32
        ).astype(jnp.bfloat16)
        scores = (
            jnp.einsum("fqc,fkc->fqk", queries, keys_all, preferred_element_type=jnp.float32)
            * score_scale
        )
        peaks = jnp.max(scores, axis=-1, keepdims=True)
        weights_exp = jnp.exp(scores - peaks)
        totals = jnp.sum(weights_exp, axis=-1)
        summed = jnp.einsum(
            "fqk,fkc->fqc",
            weights_exp.astype(jnp.bfloat16),
            values_all,
            preferred_element_type=jnp.float32,
        )
        attended = (summed / totals[:, :, None]).astype(jnp.bfloat16)
        projected = jnp.einsum(
            "ftc,cd->ftd", attended, out_weight, preferred_element_type=jnp.float32
        )
        encoded = mixed.astype(jnp.float32) + projected.reshape(mixed.shape)
        outputs.append(encoded.astype(jnp.bfloat16))
    return jnp.concatenate(outputs, axis=0)


def solution(mesh):
    in_specs = (
        P(("group", "tm"), "height", None, None),
        P(("group", "tm"), None),
        P(),
        P(),
        P(),
        P(),
        P(),
        P(),
        P(),
        P(),
    )
    out_specs = P(("group", "tm"), "height", None, None)
    return jax.shard_map(shards, mesh=mesh, in_specs=in_specs, out_specs=out_specs, check_vma=False)
```

```python
import jax
import jax.numpy as jnp
from jax import lax
from jax.sharding import PartitionSpec as P


def padded_2(cells, sides, width):
    for axis, dim in sides:
        count = lax.axis_size(axis)
        ends = count - 1
        head = lax.slice_in_dim(cells, 0, width, axis=dim)
        tail = lax.slice_in_dim(cells, cells.shape[dim] - width, cells.shape[dim], axis=dim)
        cells = jnp.concatenate(
            [
                lax.ppermute(tail, axis, [(i, (i + 1) % count) for i in range(ends)]),
                cells,
                lax.ppermute(head, axis, [((i + 1) % count, i) for i in range(ends)]),
            ],
            axis=dim,
        )
    return cells


def ring_gather(block, axis, dim):
    count = lax.axis_size(axis)
    ring = list(range(0, count, 2)) + list(range(count - 1 - count % 2, 0, -2))
    ahead = [(ring[p], ring[(p + 1) % count]) for p in range(count)]
    behind = [(ring[p], ring[(p - 1) % count]) for p in range(count)]
    pieces = [block]
    forward = block
    backward = block
    for step in range((count - 1) // 2):
        forward = lax.ppermute(forward, axis, ahead)
        backward = lax.ppermute(backward, axis, behind)
        pieces += [forward, backward]
    if count % 2 == 0 and count > 1:
        half = block.shape[dim] // 2
        front = lax.ppermute(lax.slice_in_dim(forward, 0, half, axis=dim), axis, ahead)
        back = lax.ppermute(
            lax.slice_in_dim(backward, half, block.shape[dim], axis=dim), axis, behind
        )
        pieces += [front, back]
    return pieces


def rms_scaled(frames, gain):
    widened = frames.astype(jnp.float32)
    mean_square = jnp.mean(widened * widened, axis=-1, keepdims=True)
    return widened * lax.rsqrt(mean_square + 1e-06) * gain


def shards(
    frames,
    earlier,
    gain_conv,
    conv_weight,
    conv_bias,
    gain_attn,
    query_weight,
    key_weight,
    value_weight,
    out_weight,
):
    span_count, row_count, col_count, channels = frames.shape
    rims = padded_2(frames, (("height", 1),), 1)
    rims = jnp.concatenate([rims[:, :1], rims[:, -1:]], axis=1)
    activated = jax.nn.silu(rms_scaled(frames, gain_conv)).astype(jnp.bfloat16)
    rims = jax.nn.silu(rms_scaled(rims, gain_conv)).astype(jnp.bfloat16)
    rimmed = jnp.concatenate([rims[:, :1], activated, rims[:, 1:]], axis=1)
    rimmed = jnp.pad(rimmed, ((0, 0), (0, 0), (1, 1), (0, 0)))
    ways = lax.axis_size("tm")
    mine = lax.axis_index("tm")
    pieces = [rimmed]
    for shift in range(1, ways):
        pieces.append(
            lax.ppermute(rimmed, "tm", [(i, (i + shift) % ways) for i in range(ways)])
        )
    pieces.append(jnp.zeros_like(rimmed[:1]))
    pool = jnp.concatenate(pieces, axis=0)
    blank = ways * span_count

    def slot(index):
        place = ((mine - index // span_count) % ways) * span_count + index % span_count
        return jnp.where(index >= 0, place, blank)

    own = jnp.arange(span_count, dtype=earlier.dtype)
    picks = jnp.stack([slot(earlier[:, 0]), slot(earlier[:, 1]), own], axis=1)

    def span_window_of(source, span):
        return jnp.take(source, picks[span], axis=0)[None]

    score_scale = 1.0 / channels**0.5
    outputs = []
    span_window = span_window_of(pool, 0)
    for span in range(span_count):
        accum = lax.conv_general_dilated(
            span_window,
            conv_weight,
            window_strides=(1, 1, 1),
            padding="VALID",
            dimension_numbers=("NDHWC", "DHWIO", "NDHWC"),
            preferred_element_type=jnp.float32,
        )[:, 0]
        mixed = (frames[span : span + 1].astype(jnp.float32) + accum + conv_bias).astype(
            jnp.bfloat16
        )
        normed = rms_scaled(mixed, gain_attn).astype(jnp.bfloat16)
        tokens = normed.reshape(1, row_count * col_count, channels)
        queries = jnp.einsum(
            "ftc,cd->ftd", tokens, query_weight, preferred_element_type=jnp.float32
        ).astype(jnp.bfloat16)
        pieces = ring_gather(tokens, "height", 1)
        if span + 1 < span_count:
            pieces[1], tied = lax.optimization_barrier((pieces[1], pool))
            span_window = span_window_of(tied, span + 1)
        tokens_all = jnp.concatenate(pieces, axis=1)
        keys_all = jnp.einsum(
            "ftc,cd->ftd", tokens_all, key_weight, preferred_element_type=jnp.float32
        ).astype(jnp.bfloat16)
        values_all = jnp.einsum(
            "ftc,cd->ftd", tokens_all, value_weight, preferred_element_type=jnp.float32
        ).astype(jnp.bfloat16)
        scores = (
            jnp.einsum("fqc,fkc->fqk", queries, keys_all, preferred_element_type=jnp.float32)
            * score_scale
        )
        peaks = jnp.max(scores, axis=-1, keepdims=True)
        weights_exp = jnp.exp(scores - peaks)
        totals = jnp.sum(weights_exp, axis=-1)
        summed = jnp.einsum(
            "fqk,fkc->fqc",
            weights_exp.astype(jnp.bfloat16),
            values_all,
            preferred_element_type=jnp.float32,
        )
        attended = (summed / totals[:, :, None]).astype(jnp.bfloat16)
        projected = jnp.einsum(
            "ftc,cd->ftd", attended, out_weight, preferred_element_type=jnp.float32
        )
        encoded = mixed.astype(jnp.float32) + projected.reshape(mixed.shape)
        outputs.append(encoded.astype(jnp.bfloat16))
    return jnp.concatenate(outputs, axis=0)


def solution(mesh):
    in_specs = (
        P(("group", "tm"), "height", None, None),
        P(("group", "tm"), None),
        P(),
        P(),
        P(),
        P(),
        P(),
        P(),
        P(),
        P(),
    )
    out_specs = P(("group", "tm"), "height", None, None)
    return jax.shard_map(shards, mesh=mesh, in_specs=in_specs, out_specs=out_specs, check_vma=False)
```

```python
import jax
import jax.numpy as jnp
from jax import lax
from jax.sharding import PartitionSpec as P


def padded_2(cells, sides, width):
    for axis, dim in sides:
        count = lax.axis_size(axis)
        ends = count - 1
        head = lax.slice_in_dim(cells, 0, width, axis=dim)
        tail = lax.slice_in_dim(cells, cells.shape[dim] - width, cells.shape[dim], axis=dim)
        cells = jnp.concatenate(
            [
                lax.ppermute(tail, axis, [(i, (i + 1) % count) for i in range(ends)]),
                cells,
                lax.ppermute(head, axis, [((i + 1) % count, i) for i in range(ends)]),
            ],
            axis=dim,
        )
    return cells


def ring_gather(block, axis, dim):
    count = lax.axis_size(axis)
    ring = list(range(0, count, 2)) + list(range(count - 1 - count % 2, 0, -2))
    ahead = [(ring[p], ring[(p + 1) % count]) for p in range(count)]
    behind = [(ring[p], ring[(p - 1) % count]) for p in range(count)]
    pieces = [block]
    forward = block
    backward = block
    for step in range((count - 1) // 2):
        forward = lax.ppermute(forward, axis, ahead)
        backward = lax.ppermute(backward, axis, behind)
        pieces += [forward, backward]
    if count % 2 == 0 and count > 1:
        half = block.shape[dim] // 2
        front = lax.ppermute(lax.slice_in_dim(forward, 0, half, axis=dim), axis, ahead)
        back = lax.ppermute(
            lax.slice_in_dim(backward, half, block.shape[dim], axis=dim), axis, behind
        )
        pieces += [front, back]
    return pieces


def rms_scaled(frames, gain):
    widened = frames.astype(jnp.float32)
    mean_square = jnp.mean(widened * widened, axis=-1, keepdims=True)
    return widened * lax.rsqrt(mean_square + 1e-06) * gain


def shards(
    frames,
    earlier,
    gain_conv,
    conv_weight,
    conv_bias,
    gain_attn,
    query_weight,
    key_weight,
    value_weight,
    out_weight,
):
    span_count, row_count, col_count, channels = frames.shape
    rims = padded_2(frames, (("height", 1),), 1)
    rims = jnp.concatenate([rims[:, :1], rims[:, -1:]], axis=1)
    activated = jax.nn.silu(rms_scaled(frames, gain_conv)).astype(jnp.bfloat16)
    rims = jax.nn.silu(rms_scaled(rims, gain_conv)).astype(jnp.bfloat16)
    rimmed = jnp.concatenate([rims[:, :1], activated, rims[:, 1:]], axis=1)
    rimmed = jnp.pad(rimmed, ((0, 0), (0, 0), (1, 1), (0, 0)))
    ways = lax.axis_size("tm")
    mine = lax.axis_index("tm")
    pieces = [rimmed]
    for shift in range(1, ways):
        pieces.append(
            lax.ppermute(rimmed, "tm", [(i, (i + shift) % ways) for i in range(ways)])
        )
    pieces.append(jnp.zeros_like(rimmed[:1]))
    pool = jnp.concatenate(pieces, axis=0)
    blank = ways * span_count

    def slot(index):
        place = ((mine - index // span_count) % ways) * span_count + index % span_count
        return jnp.where(index >= 0, place, blank)

    own = jnp.arange(span_count, dtype=earlier.dtype)
    picks = jnp.stack([slot(earlier[:, 0]), slot(earlier[:, 1]), own], axis=1)
    window = jnp.take(pool, picks.reshape(-1), axis=0).reshape(
        (span_count, 3) + rimmed.shape[1:]
    )
    score_scale = 1.0 / channels**0.5
    outputs = []
    span_window = window[:1]
    for span in range(span_count):
        accum = lax.conv_general_dilated(
            span_window,
            conv_weight,
            window_strides=(1, 1, 1),
            padding="VALID",
            dimension_numbers=("NDHWC", "DHWIO", "NDHWC"),
            preferred_element_type=jnp.float32,
        )[:, 0]
        mixed = (frames[span : span + 1].astype(jnp.float32) + accum + conv_bias).astype(
            jnp.bfloat16
        )
        normed = rms_scaled(mixed, gain_attn).astype(jnp.bfloat16)
        tokens = normed.reshape(1, row_count * col_count, channels)
        queries = jnp.einsum(
            "ftc,cd->ftd", tokens, query_weight, preferred_element_type=jnp.float32
        ).astype(jnp.bfloat16)
        if span > 0:
            tokens, _ = lax.optimization_barrier((tokens, previous_tail))
        pieces = ring_gather(tokens, "height", 1)
        previous_tail = pieces[-2:]
        if span + 1 < span_count:
            pieces[1], span_window = lax.optimization_barrier(
                (pieces[1], window[span + 1 : span + 2])
            )
        tokens_all = jnp.concatenate(pieces, axis=1)
        keys_all = jnp.einsum(
            "ftc,cd->ftd", tokens_all, key_weight, preferred_element_type=jnp.float32
        ).astype(jnp.bfloat16)
        values_all = jnp.einsum(
            "ftc,cd->ftd", tokens_all, value_weight, preferred_element_type=jnp.float32
        ).astype(jnp.bfloat16)
        scores = (
            jnp.einsum("fqc,fkc->fqk", queries, keys_all, preferred_element_type=jnp.float32)
            * score_scale
        )
        peaks = jnp.max(scores, axis=-1, keepdims=True)
        weights_exp = jnp.exp(scores - peaks)
        totals = jnp.sum(weights_exp, axis=-1)
        summed = jnp.einsum(
            "fqk,fkc->fqc",
            weights_exp.astype(jnp.bfloat16),
            values_all,
            preferred_element_type=jnp.float32,
        )
        attended = (summed / totals[:, :, None]).astype(jnp.bfloat16)
        projected = jnp.einsum(
            "ftc,cd->ftd", attended, out_weight, preferred_element_type=jnp.float32
        )
        encoded = mixed.astype(jnp.float32) + projected.reshape(mixed.shape)
        outputs.append(encoded.astype(jnp.bfloat16))
    return jnp.concatenate(outputs, axis=0)


def solution(mesh):
    in_specs = (
        P(("group", "tm"), "height", None, None),
        P(("group", "tm"), None),
        P(),
        P(),
        P(),
        P(),
        P(),
        P(),
        P(),
        P(),
    )
    out_specs = P(("group", "tm"), "height", None, None)
    return jax.shard_map(shards, mesh=mesh, in_specs=in_specs, out_specs=out_specs, check_vma=False)
```

```python
import jax
import jax.numpy as jnp
from jax import lax
from jax.experimental import pallas as pl
from jax.sharding import PartitionSpec as P


def padded_2(cells, sides, width):
    for axis, dim in sides:
        count = lax.axis_size(axis)
        ends = count - 1
        head = lax.slice_in_dim(cells, 0, width, axis=dim)
        tail = lax.slice_in_dim(cells, cells.shape[dim] - width, cells.shape[dim], axis=dim)
        cells = jnp.concatenate(
            [
                lax.ppermute(tail, axis, [(i, (i + 1) % count) for i in range(ends)]),
                cells,
                lax.ppermute(head, axis, [((i + 1) % count, i) for i in range(ends)]),
            ],
            axis=dim,
        )
    return cells


def ring_gather(block, axis, dim):
    count = lax.axis_size(axis)
    ring = list(range(0, count, 2)) + list(range(count - 1 - count % 2, 0, -2))
    ahead = [(ring[p], ring[(p + 1) % count]) for p in range(count)]
    behind = [(ring[p], ring[(p - 1) % count]) for p in range(count)]
    pieces = [block]
    forward = block
    backward = block
    for step in range((count - 1) // 2):
        forward = lax.ppermute(forward, axis, ahead)
        backward = lax.ppermute(backward, axis, behind)
        pieces += [forward, backward]
    if count % 2 == 0 and count > 1:
        half = block.shape[dim] // 2
        front = lax.ppermute(lax.slice_in_dim(forward, 0, half, axis=dim), axis, ahead)
        back = lax.ppermute(
            lax.slice_in_dim(backward, half, block.shape[dim], axis=dim), axis, behind
        )
        pieces += [front, back]
    return pieces


def attend_kernel(query_ref, token_ref, key_w_ref, value_w_ref, out_ref, *, scale):
    tokens = token_ref[0]
    keys = jnp.dot(tokens, key_w_ref[...], preferred_element_type=jnp.float32).astype(
        jnp.bfloat16
    )
    values = jnp.dot(tokens, value_w_ref[...], preferred_element_type=jnp.float32).astype(
        jnp.bfloat16
    )
    scores = (
        lax.dot_general(
            query_ref[0], keys, (((1,), (1,)), ((), ())), preferred_element_type=jnp.float32
        )
        * scale
    )
    peaks = jnp.max(scores, axis=-1, keepdims=True)
    weights_exp = jnp.exp(scores - peaks)
    totals = jnp.sum(weights_exp, axis=-1, keepdims=True)
    summed = jnp.dot(weights_exp.astype(jnp.bfloat16), values, preferred_element_type=jnp.float32)
    out_ref[0] = (summed / totals).astype(out_ref.dtype)


def attend(queries, tokens_all, key_weight, value_weight, scale):
    spans, query_rows, channels = queries.shape
    key_rows = tokens_all.shape[1]
    kernel = lambda *refs: attend_kernel(*refs, scale=scale)
    weight_spec = pl.BlockSpec((channels, channels), lambda f: (0, 0))
    return pl.pallas_call(
        kernel,
        grid=(spans,),
        in_specs=[
            pl.BlockSpec((1, query_rows, channels), lambda f: (f, 0, 0)),
            pl.BlockSpec((1, key_rows, channels), lambda f: (f, 0, 0)),
            weight_spec,
            weight_spec,
        ],
        out_specs=pl.BlockSpec((1, query_rows, channels), lambda f: (f, 0, 0)),
        out_shape=jax.ShapeDtypeStruct(queries.shape, jnp.bfloat16),
    )(queries, tokens_all, key_weight, value_weight)


def rms_scaled(frames, gain):
    widened = frames.astype(jnp.float32)
    mean_square = jnp.mean(widened * widened, axis=-1, keepdims=True)
    return widened * lax.rsqrt(mean_square + 1e-06) * gain


def shards(
    frames,
    earlier,
    gain_conv,
    conv_weight,
    conv_bias,
    gain_attn,
    query_weight,
    key_weight,
    value_weight,
    out_weight,
):
    span_count, row_count, col_count, channels = frames.shape
    rims = padded_2(frames, (("height", 1),), 1)
    rims = jnp.concatenate([rims[:, :1], rims[:, -1:]], axis=1)
    activated = jax.nn.silu(rms_scaled(frames, gain_conv)).astype(jnp.bfloat16)
    rims = jax.nn.silu(rms_scaled(rims, gain_conv)).astype(jnp.bfloat16)
    rimmed = jnp.concatenate([rims[:, :1], activated, rims[:, 1:]], axis=1)
    rimmed = jnp.pad(rimmed, ((0, 0), (0, 0), (1, 1), (0, 0)))
    ways = lax.axis_size("tm")
    mine = lax.axis_index("tm")
    pieces = [rimmed]
    for shift in range(1, ways):
        pieces.append(
            lax.ppermute(rimmed, "tm", [(i, (i + shift) % ways) for i in range(ways)])
        )
    pieces.append(jnp.zeros_like(rimmed[:1]))
    pool = jnp.concatenate(pieces, axis=0)
    blank = ways * span_count

    def slot(index):
        place = ((mine - index // span_count) % ways) * span_count + index % span_count
        return jnp.where(index >= 0, place, blank)

    own = jnp.arange(span_count, dtype=earlier.dtype)
    picks = jnp.stack([slot(earlier[:, 0]), slot(earlier[:, 1]), own], axis=1)
    window = jnp.take(pool, picks.reshape(-1), axis=0).reshape(
        (span_count, 3) + rimmed.shape[1:]
    )
    score_scale = 1.0 / channels**0.5
    outputs = []
    span_window = window[:1]
    for span in range(span_count):
        accum = lax.conv_general_dilated(
            span_window,
            conv_weight,
            window_strides=(1, 1, 1),
            padding="VALID",
            dimension_numbers=("NDHWC", "DHWIO", "NDHWC"),
            preferred_element_type=jnp.float32,
        )[:, 0]
        mixed = (frames[span : span + 1].astype(jnp.float32) + accum + conv_bias).astype(
            jnp.bfloat16
        )
        normed = rms_scaled(mixed, gain_attn).astype(jnp.bfloat16)
        tokens = normed.reshape(1, row_count * col_count, channels)
        queries = jnp.einsum(
            "ftc,cd->ftd", tokens, query_weight, preferred_element_type=jnp.float32
        ).astype(jnp.bfloat16)
        pieces = ring_gather(tokens, "height", 1)
        if span + 1 < span_count:
            pieces[1], span_window = lax.optimization_barrier(
                (pieces[1], window[span + 1 : span + 2])
            )
        tokens_all = jnp.concatenate(pieces, axis=1)
        attended = attend(queries, tokens_all, key_weight, value_weight, score_scale)
        projected = jnp.einsum(
            "ftc,cd->ftd", attended, out_weight, preferred_element_type=jnp.float32
        )
        encoded = mixed.astype(jnp.float32) + projected.reshape(mixed.shape)
        outputs.append(encoded.astype(jnp.bfloat16))
    return jnp.concatenate(outputs, axis=0)


def solution(mesh):
    in_specs = (
        P(("group", "tm"), "height", None, None),
        P(("group", "tm"), None),
        P(),
        P(),
        P(),
        P(),
        P(),
        P(),
        P(),
        P(),
    )
    out_specs = P(("group", "tm"), "height", None, None)
    return jax.shard_map(shards, mesh=mesh, in_specs=in_specs, out_specs=out_specs, check_vma=False)
```

```python
import jax
import jax.numpy as jnp
from jax import lax
from jax.sharding import PartitionSpec as P


def padded_2(cells, sides, width):
    for axis, dim in sides:
        count = lax.axis_size(axis)
        ends = count - 1
        head = lax.slice_in_dim(cells, 0, width, axis=dim)
        tail = lax.slice_in_dim(cells, cells.shape[dim] - width, cells.shape[dim], axis=dim)
        cells = jnp.concatenate(
            [
                lax.ppermute(tail, axis, [(i, (i + 1) % count) for i in range(ends)]),
                cells,
                lax.ppermute(head, axis, [((i + 1) % count, i) for i in range(ends)]),
            ],
            axis=dim,
        )
    return cells


def ring_gather(block, axis, dim):
    count = lax.axis_size(axis)
    ring = list(range(0, count, 2)) + list(range(count - 1 - count % 2, 0, -2))
    ahead = [(ring[p], ring[(p + 1) % count]) for p in range(count)]
    behind = [(ring[p], ring[(p - 1) % count]) for p in range(count)]
    pieces = [block]
    forward = block
    backward = block
    for step in range((count - 1) // 2):
        forward = lax.ppermute(forward, axis, ahead)
        backward = lax.ppermute(backward, axis, behind)
        pieces += [forward, backward]
    if count % 2 == 0 and count > 1:
        half = block.shape[dim] // 2
        front = lax.ppermute(lax.slice_in_dim(forward, 0, half, axis=dim), axis, ahead)
        back = lax.ppermute(
            lax.slice_in_dim(backward, half, block.shape[dim], axis=dim), axis, behind
        )
        pieces += [front, back]
    return pieces


def rms_scaled(frames, gain):
    widened = frames.astype(jnp.float32)
    mean_square = jnp.mean(widened * widened, axis=-1, keepdims=True)
    return widened * lax.rsqrt(mean_square + 1e-06) * gain


def shards(
    frames,
    earlier,
    gain_conv,
    conv_weight,
    conv_bias,
    gain_attn,
    query_weight,
    key_weight,
    value_weight,
    out_weight,
):
    span_count, row_count, col_count, channels = frames.shape
    rims = padded_2(frames, (("height", 1),), 1)
    rims = jnp.concatenate([rims[:, :1], rims[:, -1:]], axis=1)
    activated = jax.nn.silu(rms_scaled(frames, gain_conv)).astype(jnp.bfloat16)
    rims = jax.nn.silu(rms_scaled(rims, gain_conv)).astype(jnp.bfloat16)
    rimmed = jnp.concatenate([rims[:, :1], activated, rims[:, 1:]], axis=1)
    rimmed = jnp.pad(rimmed, ((0, 0), (0, 0), (1, 1), (0, 0)))
    ways = lax.axis_size("tm")
    mine = lax.axis_index("tm")
    pieces = [rimmed]
    for shift in range(1, ways):
        pieces.append(
            lax.ppermute(rimmed, "tm", [(i, (i + shift) % ways) for i in range(ways)])
        )
    pieces.append(jnp.zeros_like(rimmed[:1]))
    pool = jnp.concatenate(pieces, axis=0)
    blank = ways * span_count

    def slot(index):
        place = ((mine - index // span_count) % ways) * span_count + index % span_count
        return jnp.where(index >= 0, place, blank)

    own = jnp.arange(span_count, dtype=earlier.dtype)
    picks = jnp.stack([slot(earlier[:, 0]), slot(earlier[:, 1]), own], axis=1)
    window = jnp.take(pool, picks.reshape(-1), axis=0).reshape(
        (span_count, 3) + rimmed.shape[1:]
    )
    score_scale = 1.0 / channels**0.5
    outputs = []
    span_window = window[:1]
    for span in range(span_count):
        accum = lax.conv_general_dilated(
            span_window,
            conv_weight,
            window_strides=(1, 1, 1),
            padding="VALID",
            dimension_numbers=("NDHWC", "DHWIO", "NDHWC"),
            preferred_element_type=jnp.float32,
        )[:, 0]
        mixed = (frames[span : span + 1].astype(jnp.float32) + accum + conv_bias).astype(
            jnp.bfloat16
        )
        normed = rms_scaled(mixed, gain_attn).astype(jnp.bfloat16)
        tokens = normed.reshape(1, row_count * col_count, channels)
        queries = jnp.einsum(
            "ftc,cd->ftd", tokens, query_weight, preferred_element_type=jnp.float32
        ).astype(jnp.bfloat16)
        pieces = ring_gather(tokens, "height", 1)
        if span + 1 < span_count:
            tie = min(3, len(pieces) - 1)
            pieces[tie], span_window = lax.optimization_barrier(
                (pieces[tie], window[span + 1 : span + 2])
            )
        tokens_all = jnp.concatenate(pieces, axis=1)
        keys_all = jnp.einsum(
            "ftc,cd->ftd", tokens_all, key_weight, preferred_element_type=jnp.float32
        ).astype(jnp.bfloat16)
        values_all = jnp.einsum(
            "ftc,cd->ftd", tokens_all, value_weight, preferred_element_type=jnp.float32
        ).astype(jnp.bfloat16)
        scores = (
            jnp.einsum("fqc,fkc->fqk", queries, keys_all, preferred_element_type=jnp.float32)
            * score_scale
        )
        peaks = jnp.max(scores, axis=-1, keepdims=True)
        weights_exp = jnp.exp(scores - peaks)
        totals = jnp.sum(weights_exp, axis=-1)
        summed = jnp.einsum(
            "fqk,fkc->fqc",
            weights_exp.astype(jnp.bfloat16),
            values_all,
            preferred_element_type=jnp.float32,
        )
        attended = (summed / totals[:, :, None]).astype(jnp.bfloat16)
        projected = jnp.einsum(
            "ftc,cd->ftd", attended, out_weight, preferred_element_type=jnp.float32
        )
        encoded = mixed.astype(jnp.float32) + projected.reshape(mixed.shape)
        outputs.append(encoded.astype(jnp.bfloat16))
    return jnp.concatenate(outputs, axis=0)


def solution(mesh):
    in_specs = (
        P(("group", "tm"), "height", None, None),
        P(("group", "tm"), None),
        P(),
        P(),
        P(),
        P(),
        P(),
        P(),
        P(),
        P(),
    )
    out_specs = P(("group", "tm"), "height", None, None)
    return jax.shard_map(shards, mesh=mesh, in_specs=in_specs, out_specs=out_specs, check_vma=False)
```

```python
import jax
import jax.numpy as jnp
from jax import lax
from jax.sharding import PartitionSpec as P


def padded_2(cells, sides, width):
    for axis, dim in sides:
        count = lax.axis_size(axis)
        ends = count - 1
        head = lax.slice_in_dim(cells, 0, width, axis=dim)
        tail = lax.slice_in_dim(cells, cells.shape[dim] - width, cells.shape[dim], axis=dim)
        cells = jnp.concatenate(
            [
                lax.ppermute(tail, axis, [(i, (i + 1) % count) for i in range(ends)]),
                cells,
                lax.ppermute(head, axis, [((i + 1) % count, i) for i in range(ends)]),
            ],
            axis=dim,
        )
    return cells


def ring_gather(block, axis, dim):
    count = lax.axis_size(axis)
    ring = list(range(0, count, 2)) + list(range(count - 1 - count % 2, 0, -2))
    ahead = [(ring[p], ring[(p + 1) % count]) for p in range(count)]
    behind = [(ring[p], ring[(p - 1) % count]) for p in range(count)]
    pieces = [block]
    forward = block
    backward = block
    for step in range((count - 1) // 2):
        forward = lax.ppermute(forward, axis, ahead)
        backward = lax.ppermute(backward, axis, behind)
        pieces += [forward, backward]
    if count % 2 == 0 and count > 1:
        half = block.shape[dim] // 2
        front = lax.ppermute(lax.slice_in_dim(forward, 0, half, axis=dim), axis, ahead)
        back = lax.ppermute(
            lax.slice_in_dim(backward, half, block.shape[dim], axis=dim), axis, behind
        )
        pieces += [front, back]
    return pieces


def rms_scaled(frames, gain):
    widened = frames.astype(jnp.float32)
    mean_square = jnp.mean(widened * widened, axis=-1, keepdims=True)
    return widened * lax.rsqrt(mean_square + 1e-06) * gain


def shards(
    frames,
    earlier,
    gain_conv,
    conv_weight,
    conv_bias,
    gain_attn,
    query_weight,
    key_weight,
    value_weight,
    out_weight,
):
    span_count, row_count, col_count, channels = frames.shape
    rims = padded_2(frames, (("height", 1),), 1)
    rims = jnp.concatenate([rims[:, :1], rims[:, -1:]], axis=1)
    activated = jax.nn.silu(rms_scaled(frames, gain_conv)).astype(jnp.bfloat16)
    rims = jax.nn.silu(rms_scaled(rims, gain_conv)).astype(jnp.bfloat16)
    rimmed = jnp.concatenate([rims[:, :1], activated, rims[:, 1:]], axis=1)
    rimmed = jnp.pad(rimmed, ((0, 0), (0, 0), (1, 1), (0, 0)))
    ways = lax.axis_size("tm")
    mine = lax.axis_index("tm")
    pieces = [rimmed]
    for shift in range(1, ways):
        pieces.append(
            lax.ppermute(rimmed, "tm", [(i, (i + shift) % ways) for i in range(ways)])
        )
    pieces.append(jnp.zeros_like(rimmed[:1]))
    pool = jnp.concatenate(pieces, axis=0)
    blank = ways * span_count

    def slot(index):
        place = ((mine - index // span_count) % ways) * span_count + index % span_count
        return jnp.where(index >= 0, place, blank)

    own = jnp.arange(span_count, dtype=earlier.dtype)
    picks = jnp.stack([slot(earlier[:, 0]), slot(earlier[:, 1]), own], axis=1)
    window = jnp.take(pool, picks.reshape(-1), axis=0).reshape(
        (span_count, 3) + rimmed.shape[1:]
    )
    score_scale = 1.0 / channels**0.5
    outputs = []
    span_window = window[:1]
    for span in range(span_count):
        accum = lax.conv_general_dilated(
            span_window,
            conv_weight,
            window_strides=(1, 1, 1),
            padding="VALID",
            dimension_numbers=("NDHWC", "DHWIO", "NDHWC"),
            preferred_element_type=jnp.float32,
        )[:, 0]
        mixed = (frames[span : span + 1].astype(jnp.float32) + accum + conv_bias).astype(
            jnp.bfloat16
        )
        normed = rms_scaled(mixed, gain_attn).astype(jnp.bfloat16)
        tokens = normed.reshape(1, row_count * col_count, channels)
        queries = jnp.einsum(
            "ftc,cd->ftd", tokens, query_weight, preferred_element_type=jnp.float32
        ).astype(jnp.bfloat16)
        pieces = ring_gather(tokens, "height", 1)
        if span + 1 < span_count:
            tie = min(2, len(pieces) - 1)
            pieces[tie], span_window = lax.optimization_barrier(
                (pieces[tie], window[span + 1 : span + 2])
            )
        tokens_all = jnp.concatenate(pieces, axis=1)
        keys_all = jnp.einsum(
            "ftc,cd->ftd", tokens_all, key_weight, preferred_element_type=jnp.float32
        ).astype(jnp.bfloat16)
        values_all = jnp.einsum(
            "ftc,cd->ftd", tokens_all, value_weight, preferred_element_type=jnp.float32
        ).astype(jnp.bfloat16)
        scores = (
            jnp.einsum("fqc,fkc->fqk", queries, keys_all, preferred_element_type=jnp.float32)
            * score_scale
        )
        peaks = jnp.max(scores, axis=-1, keepdims=True)
        weights_exp = jnp.exp(scores - peaks)
        totals = jnp.sum(weights_exp, axis=-1)
        summed = jnp.einsum(
            "fqk,fkc->fqc",
            weights_exp.astype(jnp.bfloat16),
            values_all,
            preferred_element_type=jnp.float32,
        )
        attended = (summed / totals[:, :, None]).astype(jnp.bfloat16)
        projected = jnp.einsum(
            "ftc,cd->ftd", attended, out_weight, preferred_element_type=jnp.float32
        )
        encoded = mixed.astype(jnp.float32) + projected.reshape(mixed.shape)
        outputs.append(encoded.astype(jnp.bfloat16))
    return jnp.concatenate(outputs, axis=0)


def solution(mesh):
    in_specs = (
        P(("group", "tm"), "height", None, None),
        P(("group", "tm"), None),
        P(),
        P(),
        P(),
        P(),
        P(),
        P(),
        P(),
        P(),
    )
    out_specs = P(("group", "tm"), "height", None, None)
    return jax.shard_map(shards, mesh=mesh, in_specs=in_specs, out_specs=out_specs, check_vma=False)
```

```python
import jax
import jax.numpy as jnp
from jax import lax
from jax.sharding import PartitionSpec as P


def padded_2(cells, sides, width):
    for axis, dim in sides:
        count = lax.axis_size(axis)
        ends = count - 1
        head = lax.slice_in_dim(cells, 0, width, axis=dim)
        tail = lax.slice_in_dim(cells, cells.shape[dim] - width, cells.shape[dim], axis=dim)
        cells = jnp.concatenate(
            [
                lax.ppermute(tail, axis, [(i, (i + 1) % count) for i in range(ends)]),
                cells,
                lax.ppermute(head, axis, [((i + 1) % count, i) for i in range(ends)]),
            ],
            axis=dim,
        )
    return cells


def ring_gather(block, axis, dim):
    count = lax.axis_size(axis)
    ring = list(range(0, count, 2)) + list(range(count - 1 - count % 2, 0, -2))
    ahead = [(ring[p], ring[(p + 1) % count]) for p in range(count)]
    behind = [(ring[p], ring[(p - 1) % count]) for p in range(count)]
    pieces = [block]
    forward = block
    backward = block
    for step in range((count - 1) // 2):
        forward = lax.ppermute(forward, axis, ahead)
        backward = lax.ppermute(backward, axis, behind)
        pieces += [forward, backward]
    if count % 2 == 0 and count > 1:
        pieces.append(lax.ppermute(forward, axis, ahead))
    return pieces


def rms_scaled(frames, gain):
    widened = frames.astype(jnp.float32)
    mean_square = jnp.mean(widened * widened, axis=-1, keepdims=True)
    return widened * lax.rsqrt(mean_square + 1e-06) * gain


def shards(
    frames,
    earlier,
    gain_conv,
    conv_weight,
    conv_bias,
    gain_attn,
    query_weight,
    key_weight,
    value_weight,
    out_weight,
):
    span_count, row_count, col_count, channels = frames.shape
    rims = padded_2(frames, (("height", 1),), 1)
    rims = jnp.concatenate([rims[:, :1], rims[:, -1:]], axis=1)
    activated = jax.nn.silu(rms_scaled(frames, gain_conv)).astype(jnp.bfloat16)
    rims = jax.nn.silu(rms_scaled(rims, gain_conv)).astype(jnp.bfloat16)
    rimmed = jnp.concatenate([rims[:, :1], activated, rims[:, 1:]], axis=1)
    rimmed = jnp.pad(rimmed, ((0, 0), (0, 0), (1, 1), (0, 0)))
    ways = lax.axis_size("tm")
    mine = lax.axis_index("tm")
    pieces = [rimmed]
    for shift in range(1, ways):
        pieces.append(
            lax.ppermute(rimmed, "tm", [(i, (i + shift) % ways) for i in range(ways)])
        )
    pieces.append(jnp.zeros_like(rimmed[:1]))
    pool = jnp.concatenate(pieces, axis=0)
    blank = ways * span_count

    def slot(index):
        place = ((mine - index // span_count) % ways) * span_count + index % span_count
        return jnp.where(index >= 0, place, blank)

    own = jnp.arange(span_count, dtype=earlier.dtype)
    picks = jnp.stack([slot(earlier[:, 0]), slot(earlier[:, 1]), own], axis=1)
    window = jnp.take(pool, picks.reshape(-1), axis=0).reshape(
        (span_count, 3) + rimmed.shape[1:]
    )
    score_scale = 1.0 / channels**0.5
    outputs = []
    span_window = window[:1]
    for span in range(span_count):
        accum = lax.conv_general_dilated(
            span_window,
            conv_weight,
            window_strides=(1, 1, 1),
            padding="VALID",
            dimension_numbers=("NDHWC", "DHWIO", "NDHWC"),
            preferred_element_type=jnp.float32,
        )[:, 0]
        mixed = (frames[span : span + 1].astype(jnp.float32) + accum + conv_bias).astype(
            jnp.bfloat16
        )
        normed = rms_scaled(mixed, gain_attn).astype(jnp.bfloat16)
        tokens = normed.reshape(1, row_count * col_count, channels)
        queries = jnp.einsum(
            "ftc,cd->ftd", tokens, query_weight, preferred_element_type=jnp.float32
        ).astype(jnp.bfloat16)
        pieces = ring_gather(tokens, "height", 1)
        if span + 1 < span_count:
            tie = min(2, len(pieces) - 1)
            pieces[tie], span_window = lax.optimization_barrier(
                (pieces[tie], window[span + 1 : span + 2])
            )
        tokens_all = jnp.concatenate(pieces, axis=1)
        keys_all = jnp.einsum(
            "ftc,cd->ftd", tokens_all, key_weight, preferred_element_type=jnp.float32
        ).astype(jnp.bfloat16)
        values_all = jnp.einsum(
            "ftc,cd->ftd", tokens_all, value_weight, preferred_element_type=jnp.float32
        ).astype(jnp.bfloat16)
        scores = (
            jnp.einsum("fqc,fkc->fqk", queries, keys_all, preferred_element_type=jnp.float32)
            * score_scale
        )
        peaks = jnp.max(scores, axis=-1, keepdims=True)
        weights_exp = jnp.exp(scores - peaks)
        totals = jnp.sum(weights_exp, axis=-1)
        summed = jnp.einsum(
            "fqk,fkc->fqc",
            weights_exp.astype(jnp.bfloat16),
            values_all,
            preferred_element_type=jnp.float32,
        )
        attended = (summed / totals[:, :, None]).astype(jnp.bfloat16)
        projected = jnp.einsum(
            "ftc,cd->ftd", attended, out_weight, preferred_element_type=jnp.float32
        )
        encoded = mixed.astype(jnp.float32) + projected.reshape(mixed.shape)
        outputs.append(encoded.astype(jnp.bfloat16))
    return jnp.concatenate(outputs, axis=0)


def solution(mesh):
    in_specs = (
        P(("group", "tm"), "height", None, None),
        P(("group", "tm"), None),
        P(),
        P(),
        P(),
        P(),
        P(),
        P(),
        P(),
        P(),
    )
    out_specs = P(("group", "tm"), "height", None, None)
    return jax.shard_map(shards, mesh=mesh, in_specs=in_specs, out_specs=out_specs, check_vma=False)
```

```python
import jax
import jax.numpy as jnp
from jax import lax
from jax.sharding import PartitionSpec as P


def padded_2(cells, sides, width):
    for axis, dim in sides:
        count = lax.axis_size(axis)
        ends = count - 1
        head = lax.slice_in_dim(cells, 0, width, axis=dim)
        tail = lax.slice_in_dim(cells, cells.shape[dim] - width, cells.shape[dim], axis=dim)
        cells = jnp.concatenate(
            [
                lax.ppermute(tail, axis, [(i, (i + 1) % count) for i in range(ends)]),
                cells,
                lax.ppermute(head, axis, [((i + 1) % count, i) for i in range(ends)]),
            ],
            axis=dim,
        )
    return cells


def ring_gather(block, axis, dim):
    count = lax.axis_size(axis)
    ring = list(range(0, count, 2)) + list(range(count - 1 - count % 2, 0, -2))
    ahead = [(ring[p], ring[(p + 1) % count]) for p in range(count)]
    behind = [(ring[p], ring[(p - 1) % count]) for p in range(count)]
    pieces = [block]
    forward = block
    backward = block
    for step in range((count - 1) // 2):
        forward = lax.ppermute(forward, axis, ahead)
        backward = lax.ppermute(backward, axis, behind)
        pieces += [forward, backward]
    if count % 2 == 0 and count > 1:
        pieces.append(lax.ppermute(forward, axis, ahead))
    return pieces


def rms_scaled(frames, gain):
    widened = frames.astype(jnp.float32)
    mean_square = jnp.mean(widened * widened, axis=-1, keepdims=True)
    return widened * lax.rsqrt(mean_square + 1e-06) * gain


def shards(
    frames,
    earlier,
    gain_conv,
    conv_weight,
    conv_bias,
    gain_attn,
    query_weight,
    key_weight,
    value_weight,
    out_weight,
):
    span_count, row_count, col_count, channels = frames.shape
    rims = padded_2(frames, (("height", 1),), 1)
    rims = jnp.concatenate([rims[:, :1], rims[:, -1:]], axis=1)
    activated = jax.nn.silu(rms_scaled(frames, gain_conv)).astype(jnp.bfloat16)
    rims = jax.nn.silu(rms_scaled(rims, gain_conv)).astype(jnp.bfloat16)
    rimmed = jnp.concatenate([rims[:, :1], activated, rims[:, 1:]], axis=1)
    rimmed = jnp.pad(rimmed, ((0, 0), (0, 0), (1, 1), (0, 0)))
    ways = lax.axis_size("tm")
    mine = lax.axis_index("tm")
    pieces = [rimmed]
    for shift in range(1, ways):
        pieces.append(
            lax.ppermute(rimmed, "tm", [(i, (i + shift) % ways) for i in range(ways)])
        )
    pieces.append(jnp.zeros_like(rimmed[:1]))
    pool = jnp.concatenate(pieces, axis=0)
    blank = ways * span_count

    def slot(index):
        place = ((mine - index // span_count) % ways) * span_count + index % span_count
        return jnp.where(index >= 0, place, blank)

    own = jnp.arange(span_count, dtype=earlier.dtype)
    picks = jnp.stack([slot(earlier[:, 0]), slot(earlier[:, 1]), own], axis=1)
    window = jnp.take(pool, picks.reshape(-1), axis=0).reshape(
        (span_count, 3) + rimmed.shape[1:]
    )
    score_scale = 1.0 / channels**0.5
    outputs = []
    span_window = window[:1]
    for span in range(span_count):
        accum = lax.conv_general_dilated(
            span_window,
            conv_weight,
            window_strides=(1, 1, 1),
            padding="VALID",
            dimension_numbers=("NDHWC", "DHWIO", "NDHWC"),
            preferred_element_type=jnp.float32,
        )[:, 0]
        mixed = (frames[span : span + 1].astype(jnp.float32) + accum + conv_bias).astype(
            jnp.bfloat16
        )
        normed = rms_scaled(mixed, gain_attn).astype(jnp.bfloat16)
        tokens = normed.reshape(1, row_count * col_count, channels)
        queries = jnp.einsum(
            "ftc,cd->ftd", tokens, query_weight, preferred_element_type=jnp.float32
        ).astype(jnp.bfloat16)
        pieces = ring_gather(tokens, "height", 1)
        if span + 1 < span_count:
            tie = min(1, len(pieces) - 1)
            pieces[tie], span_window = lax.optimization_barrier(
                (pieces[tie], window[span + 1 : span + 2])
            )
        tokens_all = jnp.concatenate(pieces, axis=1)
        keys_all = jnp.einsum(
            "ftc,cd->ftd", tokens_all, key_weight, preferred_element_type=jnp.float32
        ).astype(jnp.bfloat16)
        values_all = jnp.einsum(
            "ftc,cd->ftd", tokens_all, value_weight, preferred_element_type=jnp.float32
        ).astype(jnp.bfloat16)
        scores = (
            jnp.einsum("fqc,fkc->fqk", queries, keys_all, preferred_element_type=jnp.float32)
            * score_scale
        )
        peaks = jnp.max(scores, axis=-1, keepdims=True)
        weights_exp = jnp.exp(scores - peaks)
        totals = jnp.sum(weights_exp, axis=-1)
        summed = jnp.einsum(
            "fqk,fkc->fqc",
            weights_exp.astype(jnp.bfloat16),
            values_all,
            preferred_element_type=jnp.float32,
        )
        attended = (summed / totals[:, :, None]).astype(jnp.bfloat16)
        projected = jnp.einsum(
            "ftc,cd->ftd", attended, out_weight, preferred_element_type=jnp.float32
        )
        encoded = mixed.astype(jnp.float32) + projected.reshape(mixed.shape)
        outputs.append(encoded.astype(jnp.bfloat16))
    return jnp.concatenate(outputs, axis=0)


def solution(mesh):
    in_specs = (
        P(("group", "tm"), "height", None, None),
        P(("group", "tm"), None),
        P(),
        P(),
        P(),
        P(),
        P(),
        P(),
        P(),
        P(),
    )
    out_specs = P(("group", "tm"), "height", None, None)
    return jax.shard_map(shards, mesh=mesh, in_specs=in_specs, out_specs=out_specs, check_vma=False)
```

```python
import jax
import jax.numpy as jnp
from jax import lax
from jax.sharding import PartitionSpec as P


def padded_2(cells, sides, width):
    for axis, dim in sides:
        count = lax.axis_size(axis)
        ends = count - 1
        head = lax.slice_in_dim(cells, 0, width, axis=dim)
        tail = lax.slice_in_dim(cells, cells.shape[dim] - width, cells.shape[dim], axis=dim)
        cells = jnp.concatenate(
            [
                lax.ppermute(tail, axis, [(i, (i + 1) % count) for i in range(ends)]),
                cells,
                lax.ppermute(head, axis, [((i + 1) % count, i) for i in range(ends)]),
            ],
            axis=dim,
        )
    return cells


def ring_gather(block, axis, dim):
    count = lax.axis_size(axis)
    ring = list(range(0, count, 2)) + list(range(count - 1 - count % 2, 0, -2))
    ahead = [(ring[p], ring[(p + 1) % count]) for p in range(count)]
    behind = [(ring[p], ring[(p - 1) % count]) for p in range(count)]
    pieces = [block]
    forward = block
    backward = block
    for step in range((count - 1) // 2):
        forward = lax.ppermute(forward, axis, ahead)
        backward = lax.ppermute(backward, axis, behind)
        pieces += [forward, backward]
    if count % 2 == 0 and count > 1:
        pieces.append(lax.ppermute(forward, axis, ahead))
    return pieces


def rms_scaled(frames, gain):
    widened = frames.astype(jnp.float32)
    mean_square = jnp.mean(widened * widened, axis=-1, keepdims=True)
    return widened * lax.rsqrt(mean_square + 1e-06) * gain


def shards(
    frames,
    earlier,
    gain_conv,
    conv_weight,
    conv_bias,
    gain_attn,
    query_weight,
    key_weight,
    value_weight,
    out_weight,
):
    span_count, row_count, col_count, channels = frames.shape
    rims = padded_2(frames, (("height", 1),), 1)
    rims = jnp.concatenate([rims[:, :1], rims[:, -1:]], axis=1)
    activated = jax.nn.silu(rms_scaled(frames, gain_conv)).astype(jnp.bfloat16)
    rims = jax.nn.silu(rms_scaled(rims, gain_conv)).astype(jnp.bfloat16)
    rimmed = jnp.concatenate([rims[:, :1], activated, rims[:, 1:]], axis=1)
    ways = lax.axis_size("tm")
    mine = lax.axis_index("tm")
    pieces = [rimmed]
    for shift in range(1, ways):
        pieces.append(
            lax.ppermute(rimmed, "tm", [(i, (i + shift) % ways) for i in range(ways)])
        )
    pieces.append(jnp.zeros_like(rimmed[:1]))
    pool = jnp.concatenate(pieces, axis=0)
    blank = ways * span_count

    def slot(index):
        place = ((mine - index // span_count) % ways) * span_count + index % span_count
        return jnp.where(index >= 0, place, blank)

    own = jnp.arange(span_count, dtype=earlier.dtype)
    picks = jnp.stack([slot(earlier[:, 0]), slot(earlier[:, 1]), own], axis=1)
    window = jnp.take(pool, picks.reshape(-1), axis=0).reshape(
        (span_count, 3) + rimmed.shape[1:]
    )
    window = jnp.pad(window, ((0, 0), (0, 0), (0, 0), (1, 1), (0, 0)))
    score_scale = 1.0 / channels**0.5
    outputs = []
    span_window = window[:1]
    for span in range(span_count):
        accum = lax.conv_general_dilated(
            span_window,
            conv_weight,
            window_strides=(1, 1, 1),
            padding="VALID",
            dimension_numbers=("NDHWC", "DHWIO", "NDHWC"),
            preferred_element_type=jnp.float32,
        )[:, 0]
        mixed = (frames[span : span + 1].astype(jnp.float32) + accum + conv_bias).astype(
            jnp.bfloat16
        )
        normed = rms_scaled(mixed, gain_attn).astype(jnp.bfloat16)
        tokens = normed.reshape(1, row_count * col_count, channels)
        queries = jnp.einsum(
            "ftc,cd->ftd", tokens, query_weight, preferred_element_type=jnp.float32
        ).astype(jnp.bfloat16)
        pieces = ring_gather(tokens, "height", 1)
        if span + 1 < span_count:
            tie = min(2, len(pieces) - 1)
            pieces[tie], span_window = lax.optimization_barrier(
                (pieces[tie], window[span + 1 : span + 2])
            )
        tokens_all = jnp.concatenate(pieces, axis=1)
        keys_all = jnp.einsum(
            "ftc,cd->ftd", tokens_all, key_weight, preferred_element_type=jnp.float32
        ).astype(jnp.bfloat16)
        values_all = jnp.einsum(
            "ftc,cd->ftd", tokens_all, value_weight, preferred_element_type=jnp.float32
        ).astype(jnp.bfloat16)
        scores = (
            jnp.einsum("fqc,fkc->fqk", queries, keys_all, preferred_element_type=jnp.float32)
            * score_scale
        )
        peaks = jnp.max(scores, axis=-1, keepdims=True)
        weights_exp = jnp.exp(scores - peaks)
        totals = jnp.sum(weights_exp, axis=-1)
        summed = jnp.einsum(
            "fqk,fkc->fqc",
            weights_exp.astype(jnp.bfloat16),
            values_all,
            preferred_element_type=jnp.float32,
        )
        attended = (summed / totals[:, :, None]).astype(jnp.bfloat16)
        projected = jnp.einsum(
            "ftc,cd->ftd", attended, out_weight, preferred_element_type=jnp.float32
        )
        encoded = mixed.astype(jnp.float32) + projected.reshape(mixed.shape)
        outputs.append(encoded.astype(jnp.bfloat16))
    return jnp.concatenate(outputs, axis=0)


def solution(mesh):
    in_specs = (
        P(("group", "tm"), "height", None, None),
        P(("group", "tm"), None),
        P(),
        P(),
        P(),
        P(),
        P(),
        P(),
        P(),
        P(),
    )
    out_specs = P(("group", "tm"), "height", None, None)
    return jax.shard_map(shards, mesh=mesh, in_specs=in_specs, out_specs=out_specs, check_vma=False)
```
